256 devices in a mesh: snd: 32 (over z, y), map: 8 (over x, core).
Axes of the slice: x: 4, y: 4, z: 8, core: 2. Of those that a mesh axis runs over, the one named last changes fastest.
Arguments:
- sensitivity_blocks: bfloat16 [32768, 128, 128], P(('snd', 'map')), may hold values from -0.125 to 0.125
- block_placement_table: int32 [3, 32768], P(None, ('snd', 'map')), may hold values from 0 to 63, as said below
- needed_tile_lists: int32 [8192, 4], P(('snd', 'map')), may hold values from -1 to 127, as said below
- location_category: int32 [65536], P('map'), may hold values from 0 to 15
- ground_warmth_celsius: float32 [64, 65536], P('snd', 'map'), may hold values from -5 to 30
- wetness_factor: float32 [64, 65536], P('snd', 'map'), may hold values from 0.2 to 1
- carbon_reservoirs: float32 [3, 65536], P(None, 'map'), may hold values from 0.2 to 3
- category_sensitivity_effect: float32 [16], replicated, may hold values from -4 to 4
- reservoir_decay_effect: float32 [3, 16], replicated, may hold values from -4 to 4
- measured_anomaly: float32 [2048, 128], P(('snd', 'map')), may hold values from -6 to 6
- retrieval_precision: float32 [2048, 128], P(('snd', 'map')), may hold values from 0.5 to 2
Outputs:
- model_xco2: float32 [2048, 128], P(('snd', 'map'))
- flux_grad: float32 [64, 65536], P('snd', 'map')
- class_grad: float32 [4, 16], replicated
- cost: float32 [], replicated
The draws below stay inside these ranges and needn't reach their ends.
Inputs may be any that keep to these rules, and one draw needn't show every extreme that they name: `block_placement_table`: row 0 is a block row below 64, row 1 a cell tile below 64, row 2 a slot below 64; each block's tile appears in its device's request list to the owner of its slot (slot // 2) as (slot % 2) * 64 + tile. `needed_tile_lists`: row o of a device's 32 rows lists distinct local tile ids of owner o followed by -1; every list has 1 to 4 ids, and on every device some list has exactly 4.
All inputs are finite; a program needn't handle non-finite values.
Results may differ from the reference program's by a relative error of at most 0.0039.
Values may be sent and summed in bfloat16 or wider, within the bound.
No kernel may reach another device: no remote copies, remote signals or barrier semaphores. Data moves between devices by JAX's collectives and lax.ppermute only.
A program may use at most 64 MiB of HBM per device.

```python
import math
import jax
import jax.numpy as jnp
from jax import lax

TILE = 128
NCLASS = 16
CAP = 4
SLOT_DEV = 2
CT_DEV = 64
BR_DEV = 64
NB_DEV = 128
EPOCH_NUMBER = 64
MAP_LOCATIONS = 65536
SROWS = 2048
NBLK = 32768
N_SND = 32
N_MAP = 8


def plan_tables(key):

    def single(dev_key):
        count_key, perm_key, row_key, full_key = jax.random.split(dev_key, 4)
        counts = jax.random.randint(count_key, (N_SND,), 1, CAP + 1)
        fullest = jax.random.randint(full_key, (), 0, N_SND)
        counts = jnp.where(jnp.arange(N_SND, dtype=jnp.int32) == fullest, CAP, counts).astype(jnp.int32)
        perm_keys = jax.random.split(perm_key, N_SND)
        orders = jax.vmap(lambda k: jax.random.permutation(k, SLOT_DEV * CT_DEV))(perm_keys).astype(jnp.int32)
        top_id = SLOT_DEV * CT_DEV - 1
        turned = (orders - orders[:, :1] + top_id) % (SLOT_DEV * CT_DEV)
        last_row = (jnp.arange(N_SND, dtype=jnp.int32) == N_SND - 1)[:, None]
        orders = jnp.where(last_row, turned, orders).astype(jnp.int32)
        chosen = orders[:, :CAP]
        live = jnp.arange(CAP, dtype=jnp.int32)[None, :] < counts[:, None]
        lists = jnp.where(live, chosen, -1)
        ends = jnp.cumsum(counts)
        total = ends[-1]
        flat = jnp.arange(NB_DEV, dtype=jnp.int32) % total
        owner = jnp.sum((ends[None, :] <= flat[:, None]).astype(jnp.int32), axis=1)
        starts = ends - counts
        within = flat - starts[owner]
        local_id = chosen[owner, within]
        slot = owner * SLOT_DEV + local_id // CT_DEV
        tile_id = local_id % CT_DEV
        rows = jax.random.randint(row_key, (NB_DEV,), 0, BR_DEV).astype(jnp.int32)
        rows = jnp.where(jnp.arange(NB_DEV, dtype=jnp.int32) == 0, BR_DEV - 1, rows).astype(jnp.int32)
        return (jnp.stack([rows, tile_id, slot]), lists)
    keys = jax.random.split(jax.random.fold_in(key, 7), N_SND * N_MAP)
    cover, lists = jax.vmap(single)(keys)
    return (cover.transpose(1, 0, 2).reshape(3, N_SND * N_MAP * NB_DEV), lists.reshape(N_SND * N_MAP * N_SND, CAP))


def draw_block_placement_table(key, part):
    return plan_tables(key)[0]


def draw_needed_tile_lists(key, part):
    return plan_tables(key)[1]


def place_ends(drawn, key, least, high):
    index_at = [jax.random.randint(jax.random.fold_in(key, axis), (), 0, length) for axis, length in enumerate(drawn.shape)]
    main_axis = drawn.shape.index(max(drawn.shape))
    beside = index_at[:main_axis] + [(index_at[main_axis] + 1) % drawn.shape[main_axis]] + index_at[main_axis + 1:]
    return drawn.at[tuple(index_at)].set(least).at[tuple(beside)].set(high)


def block_levels(stream_key, dims, shards, low, largest):
    gain, own = 1.0, jax.random.fold_in(stream_key, 6)
    for dim, shards_of in shards:
        heights = jnp.exp(jax.random.uniform(jax.random.fold_in(own, dim), (shards_of,), jnp.float32, low / len(shards), largest / len(shards)))
        gain = gain * jnp.repeat(heights, dims[dim] // shards_of).reshape([-1 if axis == dim else 1 for axis in range(len(dims))])
    return gain


def centred(rng, dims, width, most, cuts=(), kind=jnp.bfloat16):
    factor_of = block_levels(rng, dims, cuts, -0.22, 0.18) if cuts else 1.0
    values = jax.random.normal(rng, dims, jnp.float32) * width * factor_of
    return jnp.minimum(jnp.maximum(values, -most), most).astype(kind)


def setup_inputs(seed: int = 0) -> dict:
    key_of = jax.random.split(jax.random.key(seed), 12)
    return {
        "sensitivity_blocks": centred(key_of[0], (NBLK, TILE, TILE), (NB_DEV * N_MAP * TILE // BR_DEV) ** -0.5, 0.125, ((0, 256),)),
        "block_placement_table": draw_block_placement_table(jax.random.fold_in(key_of[11], 71), 0),
        "needed_tile_lists": draw_needed_tile_lists(jax.random.fold_in(key_of[11], 71), 0),
        "location_category": place_ends(jax.random.randint(key_of[3], (MAP_LOCATIONS,), 0, NCLASS), jax.random.fold_in(key_of[3], 1), 0, NCLASS - 1).astype(jnp.int32),
        "ground_warmth_celsius": jnp.clip(-5.0 + 35.0 * jax.random.uniform(key_of[4], (EPOCH_NUMBER, MAP_LOCATIONS), jnp.float32) ** block_levels(key_of[4], (EPOCH_NUMBER, MAP_LOCATIONS), ((0, 32), (1, 8)), -0.2, 0.2), -5.0, 30.0),
        "wetness_factor": jnp.clip(0.2 + 0.8 * jax.random.uniform(key_of[5], (EPOCH_NUMBER, MAP_LOCATIONS), jnp.float32) ** block_levels(key_of[5], (EPOCH_NUMBER, MAP_LOCATIONS), ((0, 32), (1, 8)), -0.2, 0.2), 0.2, 1.0),
        "carbon_reservoirs": jnp.clip(jnp.exp(math.log(3.0) - 2.7080502 * jax.random.uniform(key_of[6], (3, MAP_LOCATIONS), jnp.float32) ** block_levels(key_of[6], (3, MAP_LOCATIONS), ((1, 8),), -0.2, 0.2)), 0.2, 3.0),
        "category_sensitivity_effect": centred(key_of[7], (NCLASS,), 0.3, 4.0, (), jnp.float32),
        "reservoir_decay_effect": centred(key_of[8], (3, NCLASS), 0.3, 4.0, (), jnp.float32),
        "measured_anomaly": centred(key_of[9], (SROWS, TILE), 1.0, 6.0, ((0, 256),), jnp.float32),
        "retrieval_precision": jnp.clip(jnp.exp(math.log(2.0) - 1.3862944 * jax.random.uniform(key_of[10], (SROWS, TILE), jnp.float32) ** block_levels(key_of[10], (SROWS, TILE), ((0, 256),), -0.2, 0.2)), 0.5, 2.0),
    }


BASELINE_CELSIUS = 15.0
LOG_BASE_Q = 0.6931471805599453
PRIOR_VAR = 0.09


def ground_efflux_forward(ground_warmth_celsius, wetness_factor, carbon_reservoirs, location_category, category_sensitivity_effect, reservoir_decay_effect):
    nclass = category_sensitivity_effect.shape[0]
    category_onehot = (location_category[None, :] == jnp.arange(nclass, dtype=jnp.int32)[:, None]).astype(jnp.float32)
    log_q = LOG_BASE_Q + jnp.dot(category_sensitivity_effect[None, :], category_onehot, precision=lax.Precision.HIGHEST)[0]
    base = jnp.array([0.6, 0.25, 0.1], dtype=jnp.float32)
    rates = base[:, None] * jnp.exp(jnp.dot(reservoir_decay_effect, category_onehot, precision=lax.Precision.HIGHEST))
    decay_lifetime = (ground_warmth_celsius - BASELINE_CELSIUS) / 10.0
    modifier = jnp.exp(log_q[None, :] * decay_lifetime) * wetness_factor
    device_number = (rates * carbon_reservoirs)[:, None, :] * modifier[None]
    return category_onehot, decay_lifetime, device_number


def reference(sensitivity_blocks, block_placement_table, needed_tile_lists, location_category, ground_warmth_celsius, wetness_factor, carbon_reservoirs, category_sensitivity_effect, reservoir_decay_effect, measured_anomaly, retrieval_precision):
    category_onehot, decay_lifetime, device_number = ground_efflux_forward(ground_warmth_celsius, wetness_factor, carbon_reservoirs, location_category, category_sensitivity_effect, reservoir_decay_effect)
    flux = device_number[0] + device_number[1] + device_number[2]
    tiles = flux.astype(jnp.bfloat16).reshape(EPOCH_NUMBER, N_MAP, CT_DEV, TILE)
    ndevs = N_SND * N_MAP
    blocks = sensitivity_blocks.reshape(ndevs, NB_DEV, TILE, TILE)
    cover = block_placement_table.reshape(3, ndevs, NB_DEV).transpose(1, 0, 2)
    devs = jnp.arange(ndevs, dtype=jnp.int32)

    def forward(carry, item):
        dev, blk, cov = item
        group = dev % N_MAP
        vectors = tiles[cov[2], group, cov[1]]
        contrib = jnp.einsum('bij,bj->bi', blk.astype(jnp.float32), vectors.astype(jnp.float32))
        rows = (dev // N_MAP) * BR_DEV + cov[0]
        return carry.at[rows].add(contrib), None

    model_xco2, _ = lax.scan(forward, jnp.zeros((SROWS, TILE), jnp.float32), (devs, blocks, cover))
    diff = model_xco2 - measured_anomaly
    weighted = (diff * retrieval_precision).astype(jnp.bfloat16)

    def adjoint(carry, item):
        dev, blk, cov = item
        group = dev % N_MAP
        rows = (dev // N_MAP) * BR_DEV + cov[0]
        back = weighted[rows].astype(jnp.float32)
        grads = jnp.einsum('bij,bi->bj', blk.astype(jnp.float32), back)
        return carry.at[cov[2], group, cov[1]].add(grads), None

    grad_tiles, _ = lax.scan(adjoint, jnp.zeros((EPOCH_NUMBER, N_MAP, CT_DEV, TILE), jnp.float32), (devs, blocks, cover))
    flux_grad = grad_tiles.reshape(EPOCH_NUMBER, MAP_LOCATIONS)
    terms = jnp.stack([jnp.sum(flux_grad * flux * decay_lifetime, axis=0), jnp.sum(flux_grad * device_number[0], axis=0), jnp.sum(flux_grad * device_number[1], axis=0), jnp.sum(flux_grad * device_number[2], axis=0)])
    class_part = jnp.dot(terms, category_onehot.T, precision=lax.Precision.HIGHEST)
    prior = jnp.concatenate([category_sensitivity_effect[None, :], reservoir_decay_effect], axis=0) / PRIOR_VAR
    class_grad = class_part + prior
    cost = 0.5 * jnp.sum(retrieval_precision * diff * diff) + 0.5 * jnp.sum(category_sensitivity_effect * category_sensitivity_effect) / PRIOR_VAR + 0.5 * jnp.sum(reservoir_decay_effect * reservoir_decay_effect) / PRIOR_VAR
    return model_xco2, flux_grad, class_grad, cost
```

```python
import jax
import jax.numpy as jnp
from jax import lax
from jax.sharding import PartitionSpec as P

BASELINE_CELSIUS = 15.0
LOG_BASE_Q = 0.6931471805599453
PRIOR_VAR = 0.09


def ground_efflux_forward(
    ground_warmth_celsius,
    wetness_factor,
    carbon_reservoirs,
    location_category,
    category_sensitivity_effect,
    reservoir_decay_effect,
):
    nclass = category_sensitivity_effect.shape[0]
    category_onehot = (
        location_category[None, :] == jnp.arange(nclass, dtype=jnp.int32)[:, None]
    ).astype(jnp.float32)
    log_q = (
        LOG_BASE_Q
        + jnp.dot(
            category_sensitivity_effect[None, :], category_onehot, precision=lax.Precision.HIGHEST
        )[0]
    )
    base = jnp.array([0.6, 0.25, 0.1], dtype=jnp.float32)
    rates = base[:, None] * jnp.exp(
        jnp.dot(reservoir_decay_effect, category_onehot, precision=lax.Precision.HIGHEST)
    )
    decay_lifetime = (ground_warmth_celsius - BASELINE_CELSIUS) / 10.0
    modifier = jnp.exp(log_q[None, :] * decay_lifetime) * wetness_factor
    device_number = (rates * carbon_reservoirs)[:, None, :] * modifier[None]
    return (category_onehot, decay_lifetime, device_number)


def shards(
    sensitivity_blocks,
    block_placement_table,
    needed_tile_lists,
    location_category,
    ground_warmth_celsius,
    wetness_factor,
    carbon_reservoirs,
    category_sensitivity_effect,
    reservoir_decay_effect,
    measured_anomaly,
    retrieval_precision,
):
    tile = sensitivity_blocks.shape[1]
    epochs_each_device, locations_each_device = ground_warmth_celsius.shape
    tiles_dev = locations_each_device // tile
    local_ids = epochs_each_device * tiles_dev
    n_snd = lax.axis_size("snd")
    n_map = lax.axis_size("map")
    cap = needed_tile_lists.shape[1]
    rows_own = measured_anomaly.shape[0]
    rows_dev = rows_own * n_map
    category_onehot, decay_lifetime, device_number = ground_efflux_forward(
        ground_warmth_celsius,
        wetness_factor,
        carbon_reservoirs,
        location_category,
        category_sensitivity_effect,
        reservoir_decay_effect,
    )
    flux = device_number[0] + device_number[1] + device_number[2]
    flux_low = flux.astype(jnp.bfloat16)

    requests = lax.all_to_all(needed_tile_lists, "snd", 0, 0, tiled=True)
    live = requests >= 0
    own_tiles = flux_low.reshape(local_ids, tile)
    answer = jnp.take(own_tiles, jnp.where(live, requests, 0).reshape(-1), axis=0)
    received = lax.all_to_all(
        answer.reshape(n_snd, cap, tile), "snd", 0, 0, tiled=True
    ).reshape(n_snd * cap, tile)

    block_row = block_placement_table[0]
    block_tile = block_placement_table[1]
    block_slot = block_placement_table[2]
    owner = block_slot // epochs_each_device
    wanted = (block_slot % epochs_each_device) * tiles_dev + block_tile
    listed = jnp.take(needed_tile_lists, owner, axis=0)
    within = jnp.argmax(listed == wanted[:, None], axis=1).astype(jnp.int32)
    position = owner * cap + within
    vectors = jnp.take(received, position, axis=0)
    contrib = jnp.einsum(
        "bij,bj->bi", sensitivity_blocks, vectors, preferred_element_type=jnp.float32
    )
    row_hot = (jnp.arange(rows_dev, dtype=jnp.int32)[:, None] == block_row[None, :]).astype(
        jnp.float32
    )
    partial_rows = jnp.dot(row_hot, contrib, precision=lax.Precision.HIGHEST)

    me_map = lax.axis_index("map")
    first = me_map * rows_own
    channels = jnp.zeros((3, rows_dev, tile), jnp.float32)
    channels = channels.at[0].set(partial_rows)
    channels = lax.dynamic_update_slice(channels, measured_anomaly[None], (1, first, 0))
    channels = lax.dynamic_update_slice(channels, retrieval_precision[None], (2, first, 0))
    summed = lax.psum(channels, "map")
    model_rows = summed[0]
    weighted_rows = ((model_rows - summed[1]) * summed[2]).astype(jnp.bfloat16)
    model_xco2 = lax.dynamic_slice(model_rows, (first, 0), (rows_own, tile))
    diff = model_xco2 - measured_anomaly
    misfit = 0.5 * jnp.sum(retrieval_precision * diff * diff)

    back_rows = jnp.take(weighted_rows, block_row, axis=0)
    block_grads = jnp.einsum(
        "bij,bi->bj", sensitivity_blocks, back_rows, preferred_element_type=jnp.float32
    )
    outgoing = jax.ops.segment_sum(block_grads, position, num_segments=n_snd * cap)
    incoming = lax.all_to_all(
        outgoing.reshape(n_snd, cap, tile), "snd", 0, 0, tiled=True
    ).reshape(n_snd * cap, tile)
    target = jnp.where(live, requests, local_ids).reshape(-1)
    grad_tiles = jax.ops.segment_sum(incoming, target, num_segments=local_ids + 1)[:local_ids]
    flux_grad = grad_tiles.reshape(epochs_each_device, locations_each_device)

    terms = jnp.stack(
        [
            jnp.sum(flux_grad * flux * decay_lifetime, axis=0),
            jnp.sum(flux_grad * device_number[0], axis=0),
            jnp.sum(flux_grad * device_number[1], axis=0),
            jnp.sum(flux_grad * device_number[2], axis=0),
        ]
    )
    class_part = jnp.dot(terms, category_onehot.T, precision=lax.Precision.HIGHEST)
    nclass = class_part.shape[1]
    mine = jnp.concatenate([class_part.reshape(-1), misfit[None]])
    n_all = n_snd * n_map
    gathered = lax.all_to_all(
        jnp.broadcast_to(mine[None], (n_all, mine.shape[0])), ("snd", "map"), 0, 0, tiled=True
    )
    totals = jnp.sum(gathered, axis=0)
    class_total = totals[:-1].reshape(4, nclass)
    total_misfit = totals[-1]
    prior = (
        jnp.concatenate([category_sensitivity_effect[None, :], reservoir_decay_effect], axis=0)
        / PRIOR_VAR
    )
    class_grad = class_total + prior
    cost = (
        total_misfit
        + 0.5 * jnp.sum(category_sensitivity_effect * category_sensitivity_effect) / PRIOR_VAR
        + 0.5 * jnp.sum(reservoir_decay_effect * reservoir_decay_effect) / PRIOR_VAR
    )
    return (model_xco2, flux_grad, class_grad, cost)


def solution(mesh):
    in_specs = (
        P(("snd", "map"), None, None),
        P(None, ("snd", "map")),
        P(("snd", "map"), None),
        P("map"),
        P("snd", "map"),
        P("snd", "map"),
        P(None, "map"),
        P(),
        P(),
        P(("snd", "map"), None),
        P(("snd", "map"), None),
    )
    out_specs = (P(("snd", "map"), None), P("snd", "map"), P(), P())
    return jax.shard_map(shards, mesh=mesh, in_specs=in_specs, out_specs=out_specs, check_vma=False)
```

```python
import jax
import jax.numpy as jnp
from jax import lax
from jax.sharding import PartitionSpec as P

BASELINE_CELSIUS = 15.0
LOG_BASE_Q = 0.6931471805599453
PRIOR_VAR = 0.09


def ground_efflux_forward(
    ground_warmth_celsius,
    wetness_factor,
    carbon_reservoirs,
    location_category,
    category_sensitivity_effect,
    reservoir_decay_effect,
):
    nclass = category_sensitivity_effect.shape[0]
    category_onehot = (
        location_category[None, :] == jnp.arange(nclass, dtype=jnp.int32)[:, None]
    ).astype(jnp.float32)
    log_q = (
        LOG_BASE_Q
        + jnp.dot(
            category_sensitivity_effect[None, :], category_onehot, precision=lax.Precision.HIGHEST
        )[0]
    )
    base = jnp.array([0.6, 0.25, 0.1], dtype=jnp.float32)
    rates = base[:, None] * jnp.exp(
        jnp.dot(reservoir_decay_effect, category_onehot, precision=lax.Precision.HIGHEST)
    )
    decay_lifetime = (ground_warmth_celsius - BASELINE_CELSIUS) / 10.0
    modifier = jnp.exp(log_q[None, :] * decay_lifetime) * wetness_factor
    device_number = (rates * carbon_reservoirs)[:, None, :] * modifier[None]
    return (category_onehot, decay_lifetime, device_number)


def shards(
    sensitivity_blocks,
    block_placement_table,
    needed_tile_lists,
    location_category,
    ground_warmth_celsius,
    wetness_factor,
    carbon_reservoirs,
    category_sensitivity_effect,
    reservoir_decay_effect,
    measured_anomaly,
    retrieval_precision,
):
    tile = sensitivity_blocks.shape[1]
    epochs_each_device, locations_each_device = ground_warmth_celsius.shape
    tiles_dev = locations_each_device // tile
    local_ids = epochs_each_device * tiles_dev
    n_snd = lax.axis_size("snd")
    n_map = lax.axis_size("map")
    cap = needed_tile_lists.shape[1]
    rows_own = measured_anomaly.shape[0]
    rows_dev = rows_own * n_map
    category_onehot, decay_lifetime, device_number = ground_efflux_forward(
        ground_warmth_celsius,
        wetness_factor,
        carbon_reservoirs,
        location_category,
        category_sensitivity_effect,
        reservoir_decay_effect,
    )
    flux = device_number[0] + device_number[1] + device_number[2]
    flux_low = flux.astype(jnp.bfloat16)

    requests = lax.all_to_all(needed_tile_lists, "snd", 0, 0, tiled=True)
    live = requests >= 0
    own_tiles = flux_low.reshape(local_ids, tile)
    answer = jnp.take(own_tiles, jnp.where(live, requests, 0).reshape(-1), axis=0)
    received = lax.all_to_all(
        answer.reshape(n_snd, cap, tile), "snd", 0, 0, tiled=True
    ).reshape(n_snd * cap, tile)

    block_row = block_placement_table[0]
    block_tile = block_placement_table[1]
    block_slot = block_placement_table[2]
    owner = block_slot // epochs_each_device
    wanted = (block_slot % epochs_each_device) * tiles_dev + block_tile
    listed = jnp.take(needed_tile_lists, owner, axis=0)
    within = jnp.argmax(listed == wanted[:, None], axis=1).astype(jnp.int32)
    position = owner * cap + within
    vectors = jnp.take(received, position, axis=0)
    contrib = jnp.einsum(
        "bij,bj->bi", sensitivity_blocks, vectors, preferred_element_type=jnp.float32
    )
    row_hot = (jnp.arange(rows_dev, dtype=jnp.int32)[:, None] == block_row[None, :]).astype(
        jnp.float32
    )
    partial_rows = jnp.dot(row_hot, contrib, precision=lax.Precision.HIGHEST)

    me_map = lax.axis_index("map")
    first = me_map * rows_own
    payload = jnp.concatenate([partial_rows, measured_anomaly, retrieval_precision], axis=0)
    swapped = lax.all_to_all(
        jnp.broadcast_to(payload[None], (n_map,) + payload.shape), "map", 0, 0, tiled=True
    )
    model_rows = jnp.sum(swapped[:, :rows_dev], axis=0)
    anomaly_rows = swapped[:, rows_dev : rows_dev + rows_own].reshape(rows_dev, tile)
    precision_rows = swapped[:, rows_dev + rows_own :].reshape(rows_dev, tile)
    weighted_rows = ((model_rows - anomaly_rows) * precision_rows).astype(jnp.bfloat16)
    model_xco2 = lax.dynamic_slice(model_rows, (first, 0), (rows_own, tile))
    diff = model_xco2 - measured_anomaly
    misfit = 0.5 * jnp.sum(retrieval_precision * diff * diff)

    back_rows = jnp.take(weighted_rows, block_row, axis=0)
    block_grads = jnp.einsum(
        "bij,bi->bj", sensitivity_blocks, back_rows, preferred_element_type=jnp.float32
    )
    outgoing = jax.ops.segment_sum(block_grads, position, num_segments=n_snd * cap)
    incoming = lax.all_to_all(
        outgoing.reshape(n_snd, cap, tile), "snd", 0, 0, tiled=True
    ).reshape(n_snd * cap, tile)
    target = jnp.where(live, requests, local_ids).reshape(-1)
    grad_tiles = jax.ops.segment_sum(incoming, target, num_segments=local_ids + 1)[:local_ids]
    flux_grad = grad_tiles.reshape(epochs_each_device, locations_each_device)

    terms = jnp.stack(
        [
            jnp.sum(flux_grad * flux * decay_lifetime, axis=0),
            jnp.sum(flux_grad * device_number[0], axis=0),
            jnp.sum(flux_grad * device_number[1], axis=0),
            jnp.sum(flux_grad * device_number[2], axis=0),
        ]
    )
    class_part = jnp.dot(terms, category_onehot.T, precision=lax.Precision.HIGHEST)
    nclass = class_part.shape[1]
    mine = jnp.concatenate([class_part.reshape(-1), misfit[None]])
    n_all = n_snd * n_map
    gathered = lax.all_to_all(
        jnp.broadcast_to(mine[None], (n_all, mine.shape[0])), ("snd", "map"), 0, 0, tiled=True
    )
    totals = jnp.sum(gathered, axis=0)
    class_total = totals[:-1].reshape(4, nclass)
    total_misfit = totals[-1]
    prior = (
        jnp.concatenate([category_sensitivity_effect[None, :], reservoir_decay_effect], axis=0)
        / PRIOR_VAR
    )
    class_grad = class_total + prior
    cost = (
        total_misfit
        + 0.5 * jnp.sum(category_sensitivity_effect * category_sensitivity_effect) / PRIOR_VAR
        + 0.5 * jnp.sum(reservoir_decay_effect * reservoir_decay_effect) / PRIOR_VAR
    )
    return (model_xco2, flux_grad, class_grad, cost)


def solution(mesh):
    in_specs = (
        P(("snd", "map"), None, None),
        P(None, ("snd", "map")),
        P(("snd", "map"), None),
        P("map"),
        P("snd", "map"),
        P("snd", "map"),
        P(None, "map"),
        P(),
        P(),
        P(("snd", "map"), None),
        P(("snd", "map"), None),
    )
    out_specs = (P(("snd", "map"), None), P("snd", "map"), P(), P())
    return jax.shard_map(shards, mesh=mesh, in_specs=in_specs, out_specs=out_specs, check_vma=False)
```

```python
import jax
import jax.numpy as jnp
from jax import lax
from jax.sharding import PartitionSpec as P

BASELINE_CELSIUS = 15.0
LOG_BASE_Q = 0.6931471805599453
PRIOR_VAR = 0.09


def ground_efflux_forward(
    ground_warmth_celsius,
    wetness_factor,
    carbon_reservoirs,
    location_category,
    category_sensitivity_effect,
    reservoir_decay_effect,
):
    nclass = category_sensitivity_effect.shape[0]
    category_onehot = (
        location_category[None, :] == jnp.arange(nclass, dtype=jnp.int32)[:, None]
    ).astype(jnp.float32)
    log_q = (
        LOG_BASE_Q
        + jnp.dot(
            category_sensitivity_effect[None, :], category_onehot, precision=lax.Precision.HIGHEST
        )[0]
    )
    base = jnp.array([0.6, 0.25, 0.1], dtype=jnp.float32)
    rates = base[:, None] * jnp.exp(
        jnp.dot(reservoir_decay_effect, category_onehot, precision=lax.Precision.HIGHEST)
    )
    decay_lifetime = (ground_warmth_celsius - BASELINE_CELSIUS) / 10.0
    modifier = jnp.exp(log_q[None, :] * decay_lifetime) * wetness_factor
    device_number = (rates * carbon_reservoirs)[:, None, :] * modifier[None]
    return (category_onehot, decay_lifetime, device_number)


def shards(
    sensitivity_blocks,
    block_placement_table,
    needed_tile_lists,
    location_category,
    ground_warmth_celsius,
    wetness_factor,
    carbon_reservoirs,
    category_sensitivity_effect,
    reservoir_decay_effect,
    measured_anomaly,
    retrieval_precision,
):
    tile = sensitivity_blocks.shape[1]
    epochs_each_device, locations_each_device = ground_warmth_celsius.shape
    tiles_dev = locations_each_device // tile
    local_ids = epochs_each_device * tiles_dev
    n_snd = lax.axis_size("snd")
    n_map = lax.axis_size("map")
    cap = needed_tile_lists.shape[1]
    rows_own = measured_anomaly.shape[0]
    rows_dev = rows_own * n_map
    category_onehot, decay_lifetime, device_number = ground_efflux_forward(
        ground_warmth_celsius,
        wetness_factor,
        carbon_reservoirs,
        location_category,
        category_sensitivity_effect,
        reservoir_decay_effect,
    )
    flux = device_number[0] + device_number[1] + device_number[2]
    flux_low = flux.astype(jnp.bfloat16)

    requests = lax.all_to_all(needed_tile_lists, "snd", 0, 0, tiled=True)
    live = requests >= 0
    nclass = category_sensitivity_effect.shape[0]
    cell_class = jnp.broadcast_to(
        location_category.astype(jnp.float32)[None], (epochs_each_device, locations_each_device)
    )
    own_fields = jnp.stack(
        [
            flux_low.astype(jnp.float32),
            flux * decay_lifetime,
            device_number[0],
            device_number[1],
            device_number[2],
            cell_class,
        ]
    ).reshape(6, local_ids, tile)
    answer = jnp.take(own_fields, jnp.where(live, requests, 0).reshape(-1), axis=1)
    received = lax.all_to_all(
        answer.reshape(6, n_snd, cap, tile), "snd", 1, 1, tiled=True
    ).reshape(6, n_snd * cap, tile)

    block_row = block_placement_table[0]
    block_tile = block_placement_table[1]
    block_slot = block_placement_table[2]
    owner = block_slot // epochs_each_device
    wanted = (block_slot % epochs_each_device) * tiles_dev + block_tile
    listed = jnp.take(needed_tile_lists, owner, axis=0)
    within = jnp.argmax(listed == wanted[:, None], axis=1).astype(jnp.int32)
    position = owner * cap + within
    vectors = jnp.take(received[0], position, axis=0).astype(jnp.bfloat16)
    contrib = jnp.einsum(
        "bij,bj->bi", sensitivity_blocks, vectors, preferred_element_type=jnp.float32
    )
    row_hot = (jnp.arange(rows_dev, dtype=jnp.int32)[:, None] == block_row[None, :]).astype(
        jnp.float32
    )
    partial_rows = jnp.dot(row_hot, contrib, precision=lax.Precision.HIGHEST)

    me_map = lax.axis_index("map")
    first = me_map * rows_own
    payload = jnp.concatenate([partial_rows, measured_anomaly, retrieval_precision], axis=0)
    swapped = lax.all_to_all(
        jnp.broadcast_to(payload[None], (n_map,) + payload.shape), "map", 0, 0, tiled=True
    )
    model_rows = jnp.sum(swapped[:, :rows_dev], axis=0)
    anomaly_rows = swapped[:, rows_dev : rows_dev + rows_own].reshape(rows_dev, tile)
    precision_rows = swapped[:, rows_dev + rows_own :].reshape(rows_dev, tile)
    weighted_rows = ((model_rows - anomaly_rows) * precision_rows).astype(jnp.bfloat16)
    model_xco2 = lax.dynamic_slice(model_rows, (first, 0), (rows_own, tile))
    diff = model_xco2 - measured_anomaly
    misfit = 0.5 * jnp.sum(retrieval_precision * diff * diff)

    back_rows = jnp.take(weighted_rows, block_row, axis=0)
    block_grads = jnp.einsum(
        "bij,bi->bj", sensitivity_blocks, back_rows, preferred_element_type=jnp.float32
    )
    outgoing = jax.ops.segment_sum(block_grads, position, num_segments=n_snd * cap)

    class_hot = (
        received[5].reshape(-1)[:, None] == jnp.arange(nclass, dtype=jnp.float32)[None, :]
    ).astype(jnp.float32)
    weighted_fields = (outgoing[None] * received[1:5]).reshape(4, -1)
    class_part = jnp.dot(weighted_fields, class_hot, precision=lax.Precision.HIGHEST)
    mine = jnp.concatenate([class_part.reshape(-1), misfit[None]])
    width = mine.shape[0]
    parcel = jnp.concatenate(
        [outgoing.reshape(n_snd, cap * tile), jnp.broadcast_to(mine[None], (n_snd, width))],
        axis=1,
    )
    incoming = lax.all_to_all(parcel, "snd", 0, 0, tiled=True)
    column = jnp.sum(incoming[:, cap * tile :], axis=0)
    gathered = lax.all_to_all(
        jnp.broadcast_to(column[None], (n_map, width)), "map", 0, 0, tiled=True
    )
    totals = jnp.sum(gathered, axis=0)

    target = jnp.where(live, requests, local_ids).reshape(-1)
    grad_tiles = jax.ops.segment_sum(
        incoming[:, : cap * tile].reshape(n_snd * cap, tile), target, num_segments=local_ids + 1
    )[:local_ids]
    flux_grad = grad_tiles.reshape(epochs_each_device, locations_each_device)

    class_total = totals[:-1].reshape(4, nclass)
    total_misfit = totals[-1]
    prior = (
        jnp.concatenate([category_sensitivity_effect[None, :], reservoir_decay_effect], axis=0)
        / PRIOR_VAR
    )
    class_grad = class_total + prior
    cost = (
        total_misfit
        + 0.5 * jnp.sum(category_sensitivity_effect * category_sensitivity_effect) / PRIOR_VAR
        + 0.5 * jnp.sum(reservoir_decay_effect * reservoir_decay_effect) / PRIOR_VAR
    )
    return (model_xco2, flux_grad, class_grad, cost)


def solution(mesh):
    in_specs = (
        P(("snd", "map"), None, None),
        P(None, ("snd", "map")),
        P(("snd", "map"), None),
        P("map"),
        P("snd", "map"),
        P("snd", "map"),
        P(None, "map"),
        P(),
        P(),
        P(("snd", "map"), None),
        P(("snd", "map"), None),
    )
    out_specs = (P(("snd", "map"), None), P("snd", "map"), P(), P())
    return jax.shard_map(shards, mesh=mesh, in_specs=in_specs, out_specs=out_specs, check_vma=False)
```

```python
import jax
import jax.numpy as jnp
from jax import lax
from jax.sharding import PartitionSpec as P

BASELINE_CELSIUS = 15.0
LOG_BASE_Q = 0.6931471805599453
PRIOR_VAR = 0.09


def ground_efflux_forward(
    ground_warmth_celsius,
    wetness_factor,
    carbon_reservoirs,
    location_category,
    category_sensitivity_effect,
    reservoir_decay_effect,
):
    nclass = category_sensitivity_effect.shape[0]
    picked_q = jnp.zeros(location_category.shape, jnp.float32)
    picked_rate = jnp.zeros((3,) + location_category.shape, jnp.float32)
    for c in range(nclass):
        hit = location_category == c
        picked_q = jnp.where(hit, category_sensitivity_effect[c], picked_q)
        picked_rate = jnp.where(hit[None], reservoir_decay_effect[:, c : c + 1], picked_rate)
    log_q = LOG_BASE_Q + picked_q
    base = jnp.array([0.6, 0.25, 0.1], dtype=jnp.float32)
    rates = base[:, None] * jnp.exp(picked_rate)
    decay_lifetime = (ground_warmth_celsius - BASELINE_CELSIUS) / 10.0
    modifier = jnp.exp(log_q[None, :] * decay_lifetime) * wetness_factor
    device_number = (rates * carbon_reservoirs)[:, None, :] * modifier[None]
    return (decay_lifetime, device_number)


def shards(
    sensitivity_blocks,
    block_placement_table,
    needed_tile_lists,
    location_category,
    ground_warmth_celsius,
    wetness_factor,
    carbon_reservoirs,
    category_sensitivity_effect,
    reservoir_decay_effect,
    measured_anomaly,
    retrieval_precision,
):
    tile = sensitivity_blocks.shape[1]
    epochs_each_device, locations_each_device = ground_warmth_celsius.shape
    tiles_dev = locations_each_device // tile
    local_ids = epochs_each_device * tiles_dev
    n_snd = lax.axis_size("snd")
    n_map = lax.axis_size("map")
    cap = needed_tile_lists.shape[1]
    rows_own = measured_anomaly.shape[0]
    rows_dev = rows_own * n_map
    decay_lifetime, device_number = ground_efflux_forward(
        ground_warmth_celsius,
        wetness_factor,
        carbon_reservoirs,
        location_category,
        category_sensitivity_effect,
        reservoir_decay_effect,
    )
    flux = device_number[0] + device_number[1] + device_number[2]
    flux_low = flux.astype(jnp.bfloat16)

    requests = lax.all_to_all(needed_tile_lists, "snd", 0, 0, tiled=True)
    live = requests >= 0
    nclass = category_sensitivity_effect.shape[0]
    cell_class = jnp.broadcast_to(
        location_category.astype(jnp.float32)[None], (epochs_each_device, locations_each_device)
    )
    own_fields = jnp.stack(
        [
            flux_low.astype(jnp.float32),
            flux * decay_lifetime,
            device_number[0],
            device_number[1],
            device_number[2],
            cell_class,
        ]
    ).reshape(6, local_ids, tile)
    answer = jnp.take(own_fields, jnp.where(live, requests, 0).reshape(-1), axis=1)
    received = lax.all_to_all(
        answer.reshape(6, n_snd, cap, tile), "snd", 1, 1, tiled=True
    ).reshape(6, n_snd * cap, tile)

    block_row = block_placement_table[0]
    block_tile = block_placement_table[1]
    block_slot = block_placement_table[2]
    owner = block_slot // epochs_each_device
    wanted = (block_slot % epochs_each_device) * tiles_dev + block_tile
    listed = jnp.take(needed_tile_lists, owner, axis=0)
    within = jnp.argmax(listed == wanted[:, None], axis=1).astype(jnp.int32)
    position = owner * cap + within
    vectors = jnp.take(received[0], position, axis=0).astype(jnp.bfloat16)
    contrib = jnp.einsum(
        "bij,bj->bi", sensitivity_blocks, vectors, preferred_element_type=jnp.float32
    )
    row_hot = (jnp.arange(rows_dev, dtype=jnp.int32)[:, None] == block_row[None, :]).astype(
        jnp.float32
    )
    partial_rows = jnp.dot(row_hot, contrib, precision=lax.Precision.HIGHEST)

    me_map = lax.axis_index("map")
    first = me_map * rows_own
    payload = jnp.concatenate([partial_rows, measured_anomaly, retrieval_precision], axis=0)
    swapped = lax.all_to_all(
        jnp.broadcast_to(payload[None], (n_map,) + payload.shape), "map", 0, 0, tiled=True
    )
    model_rows = jnp.sum(swapped[:, :rows_dev], axis=0)
    anomaly_rows = swapped[:, rows_dev : rows_dev + rows_own].reshape(rows_dev, tile)
    precision_rows = swapped[:, rows_dev + rows_own :].reshape(rows_dev, tile)
    weighted_rows = ((model_rows - anomaly_rows) * precision_rows).astype(jnp.bfloat16)
    model_xco2 = lax.dynamic_slice(model_rows, (first, 0), (rows_own, tile))
    diff = model_xco2 - measured_anomaly
    misfit = 0.5 * jnp.sum(retrieval_precision * diff * diff)

    back_rows = jnp.take(weighted_rows, block_row, axis=0)
    block_grads = jnp.einsum(
        "bij,bi->bj", sensitivity_blocks, back_rows, preferred_element_type=jnp.float32
    )
    outgoing = jax.ops.segment_sum(block_grads, position, num_segments=n_snd * cap)

    class_hot = (
        received[5].reshape(-1)[:, None] == jnp.arange(nclass, dtype=jnp.float32)[None, :]
    ).astype(jnp.float32)
    weighted_fields = (outgoing[None] * received[1:5]).reshape(4, -1)
    class_part = jnp.dot(weighted_fields, class_hot, precision=lax.Precision.HIGHEST)
    mine = jnp.concatenate([class_part.reshape(-1), misfit[None]])
    width = mine.shape[0]
    parcel = jnp.concatenate(
        [outgoing.reshape(n_snd, cap * tile), jnp.broadcast_to(mine[None], (n_snd, width))],
        axis=1,
    )
    incoming = lax.all_to_all(parcel, "snd", 0, 0, tiled=True)
    column = jnp.sum(incoming[:, cap * tile :], axis=0)
    gathered = lax.all_to_all(
        jnp.broadcast_to(column[None], (n_map, width)), "map", 0, 0, tiled=True
    )
    totals = jnp.sum(gathered, axis=0)

    target = jnp.where(live, requests, local_ids).reshape(-1)
    grad_tiles = jax.ops.segment_sum(
        incoming[:, : cap * tile].reshape(n_snd * cap, tile), target, num_segments=local_ids + 1
    )[:local_ids]
    flux_grad = grad_tiles.reshape(epochs_each_device, locations_each_device)

    class_total = totals[:-1].reshape(4, nclass)
    total_misfit = totals[-1]
    prior = (
        jnp.concatenate([category_sensitivity_effect[None, :], reservoir_decay_effect], axis=0)
        / PRIOR_VAR
    )
    class_grad = class_total + prior
    cost = (
        total_misfit
        + 0.5 * jnp.sum(category_sensitivity_effect * category_sensitivity_effect) / PRIOR_VAR
        + 0.5 * jnp.sum(reservoir_decay_effect * reservoir_decay_effect) / PRIOR_VAR
    )
    return (model_xco2, flux_grad, class_grad, cost)


def solution(mesh):
    in_specs = (
        P(("snd", "map"), None, None),
        P(None, ("snd", "map")),
        P(("snd", "map"), None),
        P("map"),
        P("snd", "map"),
        P("snd", "map"),
        P(None, "map"),
        P(),
        P(),
        P(("snd", "map"), None),
        P(("snd", "map"), None),
    )
    out_specs = (P(("snd", "map"), None), P("snd", "map"), P(), P())
    return jax.shard_map(shards, mesh=mesh, in_specs=in_specs, out_specs=out_specs, check_vma=False)
```

```python
import jax
import jax.numpy as jnp
from jax import lax
from jax.sharding import PartitionSpec as P
from jax.experimental import pallas as pl
from jax.experimental.pallas import tpu as pltpu

BASELINE_CELSIUS = 15.0
LOG_BASE_Q = 0.6931471805599453
PRIOR_VAR = 0.09


def ground_efflux_forward(
    ground_warmth_celsius,
    wetness_factor,
    carbon_reservoirs,
    location_category,
    category_sensitivity_effect,
    reservoir_decay_effect,
):
    nclass = category_sensitivity_effect.shape[0]
    category_onehot = (
        location_category[None, :] == jnp.arange(nclass, dtype=jnp.int32)[:, None]
    ).astype(jnp.float32)
    log_q = (
        LOG_BASE_Q
        + jnp.dot(
            category_sensitivity_effect[None, :], category_onehot, precision=lax.Precision.HIGHEST
        )[0]
    )
    base = jnp.array([0.6, 0.25, 0.1], dtype=jnp.float32)
    rates = base[:, None] * jnp.exp(
        jnp.dot(reservoir_decay_effect, category_onehot, precision=lax.Precision.HIGHEST)
    )
    decay_lifetime = (ground_warmth_celsius - BASELINE_CELSIUS) / 10.0
    modifier = jnp.exp(log_q[None, :] * decay_lifetime) * wetness_factor
    device_number = (rates * carbon_reservoirs)[:, None, :] * modifier[None]
    return (category_onehot, decay_lifetime, device_number)


def _fields_kernel(cse_ref, rde_ref, cat_ref, warm_ref, wet_ref, carbon_ref, out_ref):
    nclass = cse_ref.shape[0]
    cat = cat_ref[...]
    picked_q = jnp.zeros(cat.shape, jnp.float32)
    picked = [jnp.zeros(cat.shape, jnp.float32) for _ in range(3)]
    for c in range(nclass):
        hit = cat == c
        picked_q = jnp.where(hit, cse_ref[c], picked_q)
        for p in range(3):
            picked[p] = jnp.where(hit, rde_ref[p * nclass + c], picked[p])
    log_q = LOG_BASE_Q + picked_q
    base = (0.6, 0.25, 0.1)
    held = [base[p] * jnp.exp(picked[p]) * carbon_ref[p] for p in range(3)]
    category = cat.astype(jnp.float32)
    for t in range(warm_ref.shape[0]):
        tau = (warm_ref[t] - BASELINE_CELSIUS) / 10.0
        modifier = jnp.exp(log_q * tau) * wet_ref[t]
        parts = [held[p] * modifier for p in range(3)]
        flux = parts[0] + parts[1] + parts[2]
        out_ref[0, t] = flux.astype(jnp.bfloat16).astype(jnp.float32)
        out_ref[1, t] = flux * tau
        out_ref[2, t] = parts[0]
        out_ref[3, t] = parts[1]
        out_ref[4, t] = parts[2]
        out_ref[5, t] = category


def owner_fields(
    ground_warmth_celsius,
    wetness_factor,
    carbon_reservoirs,
    location_category,
    category_sensitivity_effect,
    reservoir_decay_effect,
    tile,
):
    epochs, cells = ground_warmth_celsius.shape
    rows = cells // tile
    smem = pl.BlockSpec(memory_space=pltpu.SMEM)
    vmem = pl.BlockSpec(memory_space=pltpu.VMEM)
    return pl.pallas_call(
        _fields_kernel,
        out_shape=jax.ShapeDtypeStruct((6, epochs, rows, tile), jnp.float32),
        in_specs=[smem, smem, vmem, vmem, vmem, vmem],
        out_specs=vmem,
    )(
        category_sensitivity_effect,
        reservoir_decay_effect.reshape(-1),
        location_category.reshape(rows, tile),
        ground_warmth_celsius.reshape(epochs, rows, tile),
        wetness_factor.reshape(epochs, rows, tile),
        carbon_reservoirs.reshape(3, rows, tile),
    )


def shards(
    sensitivity_blocks,
    block_placement_table,
    needed_tile_lists,
    location_category,
    ground_warmth_celsius,
    wetness_factor,
    carbon_reservoirs,
    category_sensitivity_effect,
    reservoir_decay_effect,
    measured_anomaly,
    retrieval_precision,
):
    tile = sensitivity_blocks.shape[1]
    epochs_each_device, locations_each_device = ground_warmth_celsius.shape
    tiles_dev = locations_each_device // tile
    local_ids = epochs_each_device * tiles_dev
    n_snd = lax.axis_size("snd")
    n_map = lax.axis_size("map")
    cap = needed_tile_lists.shape[1]
    rows_own = measured_anomaly.shape[0]
    rows_dev = rows_own * n_map
    requests = lax.all_to_all(needed_tile_lists, "snd", 0, 0, tiled=True)
    live = requests >= 0
    nclass = category_sensitivity_effect.shape[0]
    own_fields = owner_fields(
        ground_warmth_celsius,
        wetness_factor,
        carbon_reservoirs,
        location_category,
        category_sensitivity_effect,
        reservoir_decay_effect,
        tile,
    ).reshape(6, local_ids, tile)
    answer = jnp.take(own_fields, jnp.where(live, requests, 0).reshape(-1), axis=1)
    received = lax.all_to_all(
        answer.reshape(6, n_snd, cap, tile), "snd", 1, 1, tiled=True
    ).reshape(6, n_snd * cap, tile)

    block_row = block_placement_table[0]
    block_tile = block_placement_table[1]
    block_slot = block_placement_table[2]
    owner = block_slot // epochs_each_device
    wanted = (block_slot % epochs_each_device) * tiles_dev + block_tile
    listed = jnp.take(needed_tile_lists, owner, axis=0)
    within = jnp.argmax(listed == wanted[:, None], axis=1).astype(jnp.int32)
    position = owner * cap + within
    vectors = jnp.take(received[0], position, axis=0).astype(jnp.bfloat16)
    contrib = jnp.einsum(
        "bij,bj->bi", sensitivity_blocks, vectors, preferred_element_type=jnp.float32
    )
    row_hot = (jnp.arange(rows_dev, dtype=jnp.int32)[:, None] == block_row[None, :]).astype(
        jnp.float32
    )
    partial_rows = jnp.dot(row_hot, contrib, precision=lax.Precision.HIGHEST)

    me_map = lax.axis_index("map")
    first = me_map * rows_own
    payload = jnp.concatenate([partial_rows, measured_anomaly, retrieval_precision], axis=0)
    swapped = lax.all_to_all(
        jnp.broadcast_to(payload[None], (n_map,) + payload.shape), "map", 0, 0, tiled=True
    )
    model_rows = jnp.sum(swapped[:, :rows_dev], axis=0)
    anomaly_rows = swapped[:, rows_dev : rows_dev + rows_own].reshape(rows_dev, tile)
    precision_rows = swapped[:, rows_dev + rows_own :].reshape(rows_dev, tile)
    weighted_rows = ((model_rows - anomaly_rows) * precision_rows).astype(jnp.bfloat16)
    model_xco2 = lax.dynamic_slice(model_rows, (first, 0), (rows_own, tile))
    diff = model_xco2 - measured_anomaly
    misfit = 0.5 * jnp.sum(retrieval_precision * diff * diff)

    back_rows = jnp.take(weighted_rows, block_row, axis=0)
    block_grads = jnp.einsum(
        "bij,bi->bj", sensitivity_blocks, back_rows, preferred_element_type=jnp.float32
    )
    outgoing = jax.ops.segment_sum(block_grads, position, num_segments=n_snd * cap)

    class_hot = (
        received[5].reshape(-1)[:, None] == jnp.arange(nclass, dtype=jnp.float32)[None, :]
    ).astype(jnp.float32)
    weighted_fields = (outgoing[None] * received[1:5]).reshape(4, -1)
    class_part = jnp.dot(weighted_fields, class_hot, precision=lax.Precision.HIGHEST)
    mine = jnp.concatenate([class_part.reshape(-1), misfit[None]])
    width = mine.shape[0]
    parcel = jnp.concatenate(
        [outgoing.reshape(n_snd, cap * tile), jnp.broadcast_to(mine[None], (n_snd, width))],
        axis=1,
    )
    incoming = lax.all_to_all(parcel, "snd", 0, 0, tiled=True)
    column = jnp.sum(incoming[:, cap * tile :], axis=0)
    gathered = lax.all_to_all(
        jnp.broadcast_to(column[None], (n_map, width)), "map", 0, 0, tiled=True
    )
    totals = jnp.sum(gathered, axis=0)

    target = jnp.where(live, requests, local_ids).reshape(-1)
    grad_tiles = jax.ops.segment_sum(
        incoming[:, : cap * tile].reshape(n_snd * cap, tile), target, num_segments=local_ids + 1
    )[:local_ids]
    flux_grad = grad_tiles.reshape(epochs_each_device, locations_each_device)

    class_total = totals[:-1].reshape(4, nclass)
    total_misfit = totals[-1]
    prior = (
        jnp.concatenate([category_sensitivity_effect[None, :], reservoir_decay_effect], axis=0)
        / PRIOR_VAR
    )
    class_grad = class_total + prior
    cost = (
        total_misfit
        + 0.5 * jnp.sum(category_sensitivity_effect * category_sensitivity_effect) / PRIOR_VAR
        + 0.5 * jnp.sum(reservoir_decay_effect * reservoir_decay_effect) / PRIOR_VAR
    )
    return (model_xco2, flux_grad, class_grad, cost)


def solution(mesh):
    in_specs = (
        P(("snd", "map"), None, None),
        P(None, ("snd", "map")),
        P(("snd", "map"), None),
        P("map"),
        P("snd", "map"),
        P("snd", "map"),
        P(None, "map"),
        P(),
        P(),
        P(("snd", "map"), None),
        P(("snd", "map"), None),
    )
    out_specs = (P(("snd", "map"), None), P("snd", "map"), P(), P())
    return jax.shard_map(shards, mesh=mesh, in_specs=in_specs, out_specs=out_specs, check_vma=False)
```

```python
import jax
import jax.numpy as jnp
from jax import lax
from jax.sharding import PartitionSpec as P
from jax.experimental import pallas as pl
from jax.experimental.pallas import tpu as pltpu

BASELINE_CELSIUS = 15.0
LOG_BASE_Q = 0.6931471805599453
PRIOR_VAR = 0.09


def ground_efflux_forward(
    ground_warmth_celsius,
    wetness_factor,
    carbon_reservoirs,
    location_category,
    category_sensitivity_effect,
    reservoir_decay_effect,
):
    nclass = category_sensitivity_effect.shape[0]
    category_onehot = (
        location_category[None, :] == jnp.arange(nclass, dtype=jnp.int32)[:, None]
    ).astype(jnp.float32)
    log_q = (
        LOG_BASE_Q
        + jnp.dot(
            category_sensitivity_effect[None, :], category_onehot, precision=lax.Precision.HIGHEST
        )[0]
    )
    base = jnp.array([0.6, 0.25, 0.1], dtype=jnp.float32)
    rates = base[:, None] * jnp.exp(
        jnp.dot(reservoir_decay_effect, category_onehot, precision=lax.Precision.HIGHEST)
    )
    decay_lifetime = (ground_warmth_celsius - BASELINE_CELSIUS) / 10.0
    modifier = jnp.exp(log_q[None, :] * decay_lifetime) * wetness_factor
    device_number = (rates * carbon_reservoirs)[:, None, :] * modifier[None]
    return (category_onehot, decay_lifetime, device_number)


def _fields_kernel(cse_ref, rde_ref, cat_ref, warm_ref, wet_ref, carbon_ref, out_ref):
    nclass = cse_ref.shape[0]
    cat = cat_ref[...]
    picked_q = jnp.zeros(cat.shape, jnp.float32)
    picked = [jnp.zeros(cat.shape, jnp.float32) for _ in range(3)]
    for c in range(nclass):
        hit = cat == c
        picked_q = jnp.where(hit, cse_ref[c], picked_q)
        for p in range(3):
            picked[p] = jnp.where(hit, rde_ref[p, c], picked[p])
    log_q = LOG_BASE_Q + picked_q
    base = (0.6, 0.25, 0.1)
    held = [base[p] * jnp.exp(picked[p]) * carbon_ref[p : p + 1, :] for p in range(3)]
    category = cat.astype(jnp.float32)
    for t in range(warm_ref.shape[0]):
        tau = (warm_ref[t : t + 1, :] - BASELINE_CELSIUS) / 10.0
        modifier = jnp.exp(log_q * tau) * wet_ref[t : t + 1, :]
        parts = [held[p] * modifier for p in range(3)]
        flux = parts[0] + parts[1] + parts[2]
        fields = (
            flux.astype(jnp.bfloat16).astype(jnp.float32),
            flux * tau,
            parts[0],
            parts[1],
            parts[2],
            category,
        )
        for q, value in enumerate(fields):
            out_ref[q, t : t + 1, :] = value


def owner_fields(
    ground_warmth_celsius,
    wetness_factor,
    carbon_reservoirs,
    location_category,
    category_sensitivity_effect,
    reservoir_decay_effect,
):
    epochs, cells = ground_warmth_celsius.shape
    smem = pl.BlockSpec(memory_space=pltpu.SMEM)
    vmem = pl.BlockSpec(memory_space=pltpu.VMEM)
    return pl.pallas_call(
        _fields_kernel,
        out_shape=jax.ShapeDtypeStruct((6, epochs, cells), jnp.float32),
        in_specs=[smem, smem, vmem, vmem, vmem, vmem],
        out_specs=vmem,
    )(
        category_sensitivity_effect,
        reservoir_decay_effect,
        location_category.reshape(1, cells),
        ground_warmth_celsius,
        wetness_factor,
        carbon_reservoirs,
    )


def shards(
    sensitivity_blocks,
    block_placement_table,
    needed_tile_lists,
    location_category,
    ground_warmth_celsius,
    wetness_factor,
    carbon_reservoirs,
    category_sensitivity_effect,
    reservoir_decay_effect,
    measured_anomaly,
    retrieval_precision,
):
    tile = sensitivity_blocks.shape[1]
    epochs_each_device, locations_each_device = ground_warmth_celsius.shape
    tiles_dev = locations_each_device // tile
    local_ids = epochs_each_device * tiles_dev
    n_snd = lax.axis_size("snd")
    n_map = lax.axis_size("map")
    cap = needed_tile_lists.shape[1]
    rows_own = measured_anomaly.shape[0]
    rows_dev = rows_own * n_map
    requests = lax.all_to_all(needed_tile_lists, "snd", 0, 0, tiled=True)
    live = requests >= 0
    nclass = category_sensitivity_effect.shape[0]
    own_fields = owner_fields(
        ground_warmth_celsius,
        wetness_factor,
        carbon_reservoirs,
        location_category,
        category_sensitivity_effect,
        reservoir_decay_effect,
    ).reshape(6, local_ids, tile)
    asked = (
        requests.reshape(-1)[:, None] == jnp.arange(local_ids, dtype=jnp.int32)[None, :]
    ).astype(jnp.float32)
    answer = jnp.einsum("rl,qlc->rqc", asked, own_fields, precision=lax.Precision.HIGHEST)
    received = lax.all_to_all(
        answer.reshape(n_snd, cap * 6 * tile), "snd", 0, 0, tiled=True
    ).reshape(n_snd * cap, 6, tile)

    block_row = block_placement_table[0]
    block_tile = block_placement_table[1]
    block_slot = block_placement_table[2]
    owner = block_slot // epochs_each_device
    wanted = (block_slot % epochs_each_device) * tiles_dev + block_tile
    listed = jnp.take(needed_tile_lists, owner, axis=0)
    within = jnp.argmax(listed == wanted[:, None], axis=1).astype(jnp.int32)
    position = owner * cap + within
    vectors = jnp.take(received[:, 0], position, axis=0).astype(jnp.bfloat16)
    contrib = jnp.einsum(
        "bij,bj->bi", sensitivity_blocks, vectors, preferred_element_type=jnp.float32
    )
    row_hot = (jnp.arange(rows_dev, dtype=jnp.int32)[:, None] == block_row[None, :]).astype(
        jnp.float32
    )
    partial_rows = jnp.dot(row_hot, contrib, precision=lax.Precision.HIGHEST)

    me_map = lax.axis_index("map")
    first = me_map * rows_own
    payload = jnp.concatenate([partial_rows, measured_anomaly, retrieval_precision], axis=0)
    swapped = lax.all_to_all(
        jnp.broadcast_to(payload[None], (n_map,) + payload.shape), "map", 0, 0, tiled=True
    )
    model_rows = jnp.sum(swapped[:, :rows_dev], axis=0)
    anomaly_rows = swapped[:, rows_dev : rows_dev + rows_own].reshape(rows_dev, tile)
    precision_rows = swapped[:, rows_dev + rows_own :].reshape(rows_dev, tile)
    weighted_rows = ((model_rows - anomaly_rows) * precision_rows).astype(jnp.bfloat16)
    model_xco2 = lax.dynamic_slice(model_rows, (first, 0), (rows_own, tile))
    diff = model_xco2 - measured_anomaly
    misfit = 0.5 * jnp.sum(retrieval_precision * diff * diff)

    back_rows = jnp.take(weighted_rows, block_row, axis=0)
    block_grads = jnp.einsum(
        "bij,bi->bj", sensitivity_blocks, back_rows, preferred_element_type=jnp.float32
    )
    outgoing = jax.ops.segment_sum(block_grads, position, num_segments=n_snd * cap)

    class_hot = (
        received[:, 5][:, :, None] == jnp.arange(nclass, dtype=jnp.float32)[None, None, :]
    ).astype(jnp.float32)
    weighted_fields = outgoing[:, None, :] * received[:, 1:5]
    class_part = jnp.einsum(
        "pqc,pck->qk", weighted_fields, class_hot, precision=lax.Precision.HIGHEST
    )
    mine = jnp.concatenate([class_part.reshape(-1), misfit[None]])
    width = mine.shape[0]
    parcel = jnp.concatenate(
        [outgoing.reshape(n_snd, cap * tile), jnp.broadcast_to(mine[None], (n_snd, width))],
        axis=1,
    )
    incoming = lax.all_to_all(parcel, "snd", 0, 0, tiled=True)
    column = jnp.sum(incoming[:, cap * tile :], axis=0)
    gathered = lax.all_to_all(
        jnp.broadcast_to(column[None], (n_map, width)), "map", 0, 0, tiled=True
    )
    totals = jnp.sum(gathered, axis=0)

    target = jnp.where(live, requests, local_ids).reshape(-1)
    grad_tiles = jax.ops.segment_sum(
        incoming[:, : cap * tile].reshape(n_snd * cap, tile), target, num_segments=local_ids + 1
    )[:local_ids]
    flux_grad = grad_tiles.reshape(epochs_each_device, locations_each_device)

    class_total = totals[:-1].reshape(4, nclass)
    total_misfit = totals[-1]
    prior = (
        jnp.concatenate([category_sensitivity_effect[None, :], reservoir_decay_effect], axis=0)
        / PRIOR_VAR
    )
    class_grad = class_total + prior
    cost = (
        total_misfit
        + 0.5 * jnp.sum(category_sensitivity_effect * category_sensitivity_effect) / PRIOR_VAR
        + 0.5 * jnp.sum(reservoir_decay_effect * reservoir_decay_effect) / PRIOR_VAR
    )
    return (model_xco2, flux_grad, class_grad, cost)


def solution(mesh):
    in_specs = (
        P(("snd", "map"), None, None),
        P(None, ("snd", "map")),
        P(("snd", "map"), None),
        P("map"),
        P("snd", "map"),
        P("snd", "map"),
        P(None, "map"),
        P(),
        P(),
        P(("snd", "map"), None),
        P(("snd", "map"), None),
    )
    out_specs = (P(("snd", "map"), None), P("snd", "map"), P(), P())
    return jax.shard_map(shards, mesh=mesh, in_specs=in_specs, out_specs=out_specs, check_vma=False)
```

```python
import jax
import jax.numpy as jnp
from jax import lax
from jax.sharding import PartitionSpec as P
from jax.experimental import pallas as pl
from jax.experimental.pallas import tpu as pltpu

BASELINE_CELSIUS = 15.0
LOG_BASE_Q = 0.6931471805599453
PRIOR_VAR = 0.09


def ground_efflux_forward(
    ground_warmth_celsius,
    wetness_factor,
    carbon_reservoirs,
    location_category,
    category_sensitivity_effect,
    reservoir_decay_effect,
):
    nclass = category_sensitivity_effect.shape[0]
    category_onehot = (
        location_category[None, :] == jnp.arange(nclass, dtype=jnp.int32)[:, None]
    ).astype(jnp.float32)
    log_q = (
        LOG_BASE_Q
        + jnp.dot(
            category_sensitivity_effect[None, :], category_onehot, precision=lax.Precision.HIGHEST
        )[0]
    )
    base = jnp.array([0.6, 0.25, 0.1], dtype=jnp.float32)
    rates = base[:, None] * jnp.exp(
        jnp.dot(reservoir_decay_effect, category_onehot, precision=lax.Precision.HIGHEST)
    )
    decay_lifetime = (ground_warmth_celsius - BASELINE_CELSIUS) / 10.0
    modifier = jnp.exp(log_q[None, :] * decay_lifetime) * wetness_factor
    device_number = (rates * carbon_reservoirs)[:, None, :] * modifier[None]
    return (category_onehot, decay_lifetime, device_number)


def _fields_kernel(cse_ref, rde_ref, cat_ref, warm_ref, wet_ref, carbon_ref, out_ref):
    nclass = cse_ref.shape[0]
    cat = cat_ref[...]
    picked_q = jnp.zeros(cat.shape, jnp.float32)
    picked = [jnp.zeros(cat.shape, jnp.float32) for _ in range(3)]
    for c in range(nclass):
        hit = cat == c
        picked_q = jnp.where(hit, cse_ref[c], picked_q)
        for p in range(3):
            picked[p] = jnp.where(hit, rde_ref[p, c], picked[p])
    log_q = LOG_BASE_Q + picked_q
    base = (0.6, 0.25, 0.1)
    held = [base[p] * jnp.exp(picked[p]) * carbon_ref[p : p + 1, :] for p in range(3)]
    category = cat.astype(jnp.float32)
    for t in range(warm_ref.shape[0]):
        tau = (warm_ref[t : t + 1, :] - BASELINE_CELSIUS) / 10.0
        modifier = jnp.exp(log_q * tau) * wet_ref[t : t + 1, :]
        parts = [held[p] * modifier for p in range(3)]
        flux = parts[0] + parts[1] + parts[2]
        fields = (
            flux.astype(jnp.bfloat16).astype(jnp.float32),
            flux * tau,
            parts[0],
            parts[1],
            parts[2],
            category,
        )
        for q, value in enumerate(fields):
            out_ref[q, t : t + 1, :] = value


def owner_fields(
    ground_warmth_celsius,
    wetness_factor,
    carbon_reservoirs,
    location_category,
    category_sensitivity_effect,
    reservoir_decay_effect,
):
    epochs, cells = ground_warmth_celsius.shape
    smem = pl.BlockSpec(memory_space=pltpu.SMEM)
    vmem = pl.BlockSpec(memory_space=pltpu.VMEM)
    return pl.pallas_call(
        _fields_kernel,
        out_shape=jax.ShapeDtypeStruct((6, epochs, cells), jnp.float32),
        in_specs=[smem, smem, vmem, vmem, vmem, vmem],
        out_specs=vmem,
    )(
        category_sensitivity_effect,
        reservoir_decay_effect,
        location_category.reshape(1, cells),
        ground_warmth_celsius,
        wetness_factor,
        carbon_reservoirs,
    )


def shards(
    sensitivity_blocks,
    block_placement_table,
    needed_tile_lists,
    location_category,
    ground_warmth_celsius,
    wetness_factor,
    carbon_reservoirs,
    category_sensitivity_effect,
    reservoir_decay_effect,
    measured_anomaly,
    retrieval_precision,
):
    tile = sensitivity_blocks.shape[1]
    epochs_each_device, locations_each_device = ground_warmth_celsius.shape
    tiles_dev = locations_each_device // tile
    local_ids = epochs_each_device * tiles_dev
    n_snd = lax.axis_size("snd")
    n_map = lax.axis_size("map")
    cap = needed_tile_lists.shape[1]
    rows_own = measured_anomaly.shape[0]
    rows_dev = rows_own * n_map
    requests = lax.all_to_all(needed_tile_lists, "snd", 0, 0, tiled=True)
    live = requests >= 0
    nclass = category_sensitivity_effect.shape[0]
    own_fields = owner_fields(
        ground_warmth_celsius,
        wetness_factor,
        carbon_reservoirs,
        location_category,
        category_sensitivity_effect,
        reservoir_decay_effect,
    ).reshape(6, local_ids, tile)
    asked = (
        requests.reshape(-1)[:, None] == jnp.arange(local_ids, dtype=jnp.int32)[None, :]
    ).astype(jnp.float32)
    answer = jnp.einsum("rl,qlc->rqc", asked, own_fields, precision=lax.Precision.HIGHEST)
    answer, block_placement_table, needed_tile_lists = lax.optimization_barrier(
        (answer, block_placement_table, needed_tile_lists)
    )
    received = lax.all_to_all(
        answer.reshape(n_snd, cap * 6 * tile), "snd", 0, 0, tiled=True
    ).reshape(n_snd * cap, 6, tile)

    block_row = block_placement_table[0]
    block_tile = block_placement_table[1]
    block_slot = block_placement_table[2]
    owner = block_slot // epochs_each_device
    wanted = (block_slot % epochs_each_device) * tiles_dev + block_tile
    listed = jnp.take(needed_tile_lists, owner, axis=0)
    within = jnp.argmax(listed == wanted[:, None], axis=1).astype(jnp.int32)
    position = owner * cap + within
    vectors = jnp.take(received[:, 0], position, axis=0).astype(jnp.bfloat16)
    contrib = jnp.einsum(
        "bij,bj->bi", sensitivity_blocks, vectors, preferred_element_type=jnp.float32
    )
    row_hot = (jnp.arange(rows_dev, dtype=jnp.int32)[:, None] == block_row[None, :]).astype(
        jnp.float32
    )
    partial_rows = jnp.dot(row_hot, contrib, precision=lax.Precision.HIGHEST)

    me_map = lax.axis_index("map")
    first = me_map * rows_own
    payload = jnp.concatenate([partial_rows, measured_anomaly, retrieval_precision], axis=0)
    swapped = lax.all_to_all(
        jnp.broadcast_to(payload[None], (n_map,) + payload.shape), "map", 0, 0, tiled=True
    )
    model_rows = jnp.sum(swapped[:, :rows_dev], axis=0)
    anomaly_rows = swapped[:, rows_dev : rows_dev + rows_own].reshape(rows_dev, tile)
    precision_rows = swapped[:, rows_dev + rows_own :].reshape(rows_dev, tile)
    weighted_rows = ((model_rows - anomaly_rows) * precision_rows).astype(jnp.bfloat16)
    model_xco2 = lax.dynamic_slice(model_rows, (first, 0), (rows_own, tile))
    diff = model_xco2 - measured_anomaly
    misfit = 0.5 * jnp.sum(retrieval_precision * diff * diff)

    back_rows = jnp.take(weighted_rows, block_row, axis=0)
    block_grads = jnp.einsum(
        "bij,bi->bj", sensitivity_blocks, back_rows, preferred_element_type=jnp.float32
    )
    outgoing = jax.ops.segment_sum(block_grads, position, num_segments=n_snd * cap)

    class_hot = (
        received[:, 5][:, :, None] == jnp.arange(nclass, dtype=jnp.float32)[None, None, :]
    ).astype(jnp.float32)
    weighted_fields = outgoing[:, None, :] * received[:, 1:5]
    class_part = jnp.einsum(
        "pqc,pck->qk", weighted_fields, class_hot, precision=lax.Precision.HIGHEST
    )
    mine = jnp.concatenate([class_part.reshape(-1), misfit[None]])
    width = mine.shape[0]
    parcel = jnp.concatenate(
        [outgoing.reshape(n_snd, cap * tile), jnp.broadcast_to(mine[None], (n_snd, width))],
        axis=1,
    )
    incoming = lax.all_to_all(parcel, "snd", 0, 0, tiled=True)
    column = jnp.sum(incoming[:, cap * tile :], axis=0)
    gathered = lax.all_to_all(
        jnp.broadcast_to(column[None], (n_map, width)), "map", 0, 0, tiled=True
    )
    totals = jnp.sum(gathered, axis=0)

    target = jnp.where(live, requests, local_ids).reshape(-1)
    grad_tiles = jax.ops.segment_sum(
        incoming[:, : cap * tile].reshape(n_snd * cap, tile), target, num_segments=local_ids + 1
    )[:local_ids]
    flux_grad = grad_tiles.reshape(epochs_each_device, locations_each_device)

    class_total = totals[:-1].reshape(4, nclass)
    total_misfit = totals[-1]
    prior = (
        jnp.concatenate([category_sensitivity_effect[None, :], reservoir_decay_effect], axis=0)
        / PRIOR_VAR
    )
    class_grad = class_total + prior
    cost = (
        total_misfit
        + 0.5 * jnp.sum(category_sensitivity_effect * category_sensitivity_effect) / PRIOR_VAR
        + 0.5 * jnp.sum(reservoir_decay_effect * reservoir_decay_effect) / PRIOR_VAR
    )
    return (model_xco2, flux_grad, class_grad, cost)


def solution(mesh):
    in_specs = (
        P(("snd", "map"), None, None),
        P(None, ("snd", "map")),
        P(("snd", "map"), None),
        P("map"),
        P("snd", "map"),
        P("snd", "map"),
        P(None, "map"),
        P(),
        P(),
        P(("snd", "map"), None),
        P(("snd", "map"), None),
    )
    out_specs = (P(("snd", "map"), None), P("snd", "map"), P(), P())
    return jax.shard_map(shards, mesh=mesh, in_specs=in_specs, out_specs=out_specs, check_vma=False)
```

```python
import jax
import jax.numpy as jnp
from jax import lax
from jax.sharding import PartitionSpec as P
from jax.experimental import pallas as pl
from jax.experimental.pallas import tpu as pltpu

BASELINE_CELSIUS = 15.0
LOG_BASE_Q = 0.6931471805599453
PRIOR_VAR = 0.09


def ground_efflux_forward(
    ground_warmth_celsius,
    wetness_factor,
    carbon_reservoirs,
    location_category,
    category_sensitivity_effect,
    reservoir_decay_effect,
):
    nclass = category_sensitivity_effect.shape[0]
    category_onehot = (
        location_category[None, :] == jnp.arange(nclass, dtype=jnp.int32)[:, None]
    ).astype(jnp.float32)
    log_q = (
        LOG_BASE_Q
        + jnp.dot(
            category_sensitivity_effect[None, :], category_onehot, precision=lax.Precision.HIGHEST
        )[0]
    )
    base = jnp.array([0.6, 0.25, 0.1], dtype=jnp.float32)
    rates = base[:, None] * jnp.exp(
        jnp.dot(reservoir_decay_effect, category_onehot, precision=lax.Precision.HIGHEST)
    )
    decay_lifetime = (ground_warmth_celsius - BASELINE_CELSIUS) / 10.0
    modifier = jnp.exp(log_q[None, :] * decay_lifetime) * wetness_factor
    device_number = (rates * carbon_reservoirs)[:, None, :] * modifier[None]
    return (category_onehot, decay_lifetime, device_number)


def _fields_kernel(cse_ref, rde_ref, cat_ref, warm_ref, wet_ref, carbon_ref, out_ref):
    nclass = cse_ref.shape[0]
    cat = cat_ref[...]
    picked_q = jnp.zeros(cat.shape, jnp.float32)
    picked = [jnp.zeros(cat.shape, jnp.float32) for _ in range(3)]
    for c in range(nclass):
        hit = cat == c
        picked_q = jnp.where(hit, cse_ref[c], picked_q)
        for p in range(3):
            picked[p] = jnp.where(hit, rde_ref[p, c], picked[p])
    log_q = LOG_BASE_Q + picked_q
    base = (0.6, 0.25, 0.1)
    held = [base[p] * jnp.exp(picked[p]) * carbon_ref[p : p + 1, :] for p in range(3)]
    category = cat.astype(jnp.float32)
    for t in range(warm_ref.shape[0]):
        tau = (warm_ref[t : t + 1, :] - BASELINE_CELSIUS) / 10.0
        modifier = jnp.exp(log_q * tau) * wet_ref[t : t + 1, :]
        parts = [held[p] * modifier for p in range(3)]
        flux = parts[0] + parts[1] + parts[2]
        fields = (
            flux.astype(jnp.bfloat16).astype(jnp.float32),
            flux * tau,
            parts[0],
            parts[1],
            parts[2],
            category,
        )
        for q, value in enumerate(fields):
            out_ref[q, t : t + 1, :] = value


def owner_fields(
    ground_warmth_celsius,
    wetness_factor,
    carbon_reservoirs,
    location_category,
    category_sensitivity_effect,
    reservoir_decay_effect,
):
    epochs, cells = ground_warmth_celsius.shape
    smem = pl.BlockSpec(memory_space=pltpu.SMEM)
    vmem = pl.BlockSpec(memory_space=pltpu.VMEM)
    return pl.pallas_call(
        _fields_kernel,
        out_shape=jax.ShapeDtypeStruct((6, epochs, cells), jnp.float32),
        in_specs=[smem, smem, vmem, vmem, vmem, vmem],
        out_specs=vmem,
    )(
        category_sensitivity_effect,
        reservoir_decay_effect,
        location_category.reshape(1, cells),
        ground_warmth_celsius,
        wetness_factor,
        carbon_reservoirs,
    )


def shards(
    sensitivity_blocks,
    block_placement_table,
    needed_tile_lists,
    location_category,
    ground_warmth_celsius,
    wetness_factor,
    carbon_reservoirs,
    category_sensitivity_effect,
    reservoir_decay_effect,
    measured_anomaly,
    retrieval_precision,
):
    tile = sensitivity_blocks.shape[1]
    epochs_each_device, locations_each_device = ground_warmth_celsius.shape
    tiles_dev = locations_each_device // tile
    local_ids = epochs_each_device * tiles_dev
    n_snd = lax.axis_size("snd")
    n_map = lax.axis_size("map")
    cap = needed_tile_lists.shape[1]
    rows_own = measured_anomaly.shape[0]
    rows_dev = rows_own * n_map
    requests = lax.all_to_all(needed_tile_lists, "snd", 0, 0)
    live = requests >= 0
    nclass = category_sensitivity_effect.shape[0]
    own_fields = owner_fields(
        ground_warmth_celsius,
        wetness_factor,
        carbon_reservoirs,
        location_category,
        category_sensitivity_effect,
        reservoir_decay_effect,
    ).reshape(6, local_ids, tile)
    asked = (
        requests.reshape(-1)[:, None] == jnp.arange(local_ids, dtype=jnp.int32)[None, :]
    ).astype(jnp.float32)
    answer = jnp.einsum("rl,qlc->rqc", asked, own_fields, precision=lax.Precision.HIGHEST)
    answer, block_placement_table, needed_tile_lists = lax.optimization_barrier(
        (answer, block_placement_table, needed_tile_lists)
    )
    received = lax.all_to_all(answer.reshape(n_snd, cap * 6, tile), "snd", 0, 0).reshape(
        n_snd * cap, 6, tile
    )

    block_row = block_placement_table[0]
    block_tile = block_placement_table[1]
    block_slot = block_placement_table[2]
    owner = block_slot // epochs_each_device
    wanted = (block_slot % epochs_each_device) * tiles_dev + block_tile
    listed = jnp.take(needed_tile_lists, owner, axis=0)
    within = jnp.argmax(listed == wanted[:, None], axis=1).astype(jnp.int32)
    position = owner * cap + within
    vectors = jnp.take(received[:, 0], position, axis=0).astype(jnp.bfloat16)
    contrib = jnp.einsum(
        "bij,bj->bi", sensitivity_blocks, vectors, preferred_element_type=jnp.float32
    )
    row_hot = (jnp.arange(rows_dev, dtype=jnp.int32)[:, None] == block_row[None, :]).astype(
        jnp.float32
    )
    partial_rows = jnp.dot(row_hot, contrib, precision=lax.Precision.HIGHEST)

    me_map = lax.axis_index("map")
    first = me_map * rows_own
    payload = jnp.concatenate([partial_rows, measured_anomaly, retrieval_precision], axis=0)
    swapped = lax.all_to_all(
        jnp.broadcast_to(payload[None], (n_map,) + payload.shape), "map", 0, 0
    )
    model_rows = jnp.sum(swapped[:, :rows_dev], axis=0)
    anomaly_rows = swapped[:, rows_dev : rows_dev + rows_own].reshape(rows_dev, tile)
    precision_rows = swapped[:, rows_dev + rows_own :].reshape(rows_dev, tile)
    weighted_rows = ((model_rows - anomaly_rows) * precision_rows).astype(jnp.bfloat16)
    model_xco2 = lax.dynamic_slice(model_rows, (first, 0), (rows_own, tile))
    diff = model_xco2 - measured_anomaly
    misfit = 0.5 * jnp.sum(retrieval_precision * diff * diff)

    back_rows = jnp.take(weighted_rows, block_row, axis=0)
    block_grads = jnp.einsum(
        "bij,bi->bj", sensitivity_blocks, back_rows, preferred_element_type=jnp.float32
    )
    outgoing = jax.ops.segment_sum(block_grads, position, num_segments=n_snd * cap)

    class_hot = (
        received[:, 5][:, :, None] == jnp.arange(nclass, dtype=jnp.float32)[None, None, :]
    ).astype(jnp.float32)
    weighted_fields = outgoing[:, None, :] * received[:, 1:5]
    class_part = jnp.einsum(
        "pqc,pck->qk", weighted_fields, class_hot, precision=lax.Precision.HIGHEST
    )
    mine = jnp.concatenate([class_part.reshape(-1), misfit[None]])
    width = mine.shape[0]
    mine = jnp.pad(mine, (0, tile - width))
    parcel = jnp.concatenate(
        [
            outgoing.reshape(n_snd, cap, tile),
            jnp.broadcast_to(mine[None, None], (n_snd, 1, tile)),
        ],
        axis=1,
    )
    incoming = lax.all_to_all(parcel, "snd", 0, 0)
    column = jnp.sum(incoming[:, cap], axis=0)
    gathered = lax.all_to_all(jnp.broadcast_to(column[None], (n_map, tile)), "map", 0, 0)
    totals = jnp.sum(gathered, axis=0)[:width]

    target = jnp.where(live, requests, local_ids).reshape(-1)
    grad_tiles = jax.ops.segment_sum(
        incoming[:, :cap].reshape(n_snd * cap, tile), target, num_segments=local_ids + 1
    )[:local_ids]
    flux_grad = grad_tiles.reshape(epochs_each_device, locations_each_device)

    class_total = totals[:-1].reshape(4, nclass)
    total_misfit = totals[-1]
    prior = (
        jnp.concatenate([category_sensitivity_effect[None, :], reservoir_decay_effect], axis=0)
        / PRIOR_VAR
    )
    class_grad = class_total + prior
    cost = (
        total_misfit
        + 0.5 * jnp.sum(category_sensitivity_effect * category_sensitivity_effect) / PRIOR_VAR
        + 0.5 * jnp.sum(reservoir_decay_effect * reservoir_decay_effect) / PRIOR_VAR
    )
    return (model_xco2, flux_grad, class_grad, cost)


def solution(mesh):
    in_specs = (
        P(("snd", "map"), None, None),
        P(None, ("snd", "map")),
        P(("snd", "map"), None),
        P("map"),
        P("snd", "map"),
        P("snd", "map"),
        P(None, "map"),
        P(),
        P(),
        P(("snd", "map"), None),
        P(("snd", "map"), None),
    )
    out_specs = (P(("snd", "map"), None), P("snd", "map"), P(), P())
    return jax.shard_map(shards, mesh=mesh, in_specs=in_specs, out_specs=out_specs, check_vma=False)
```

```python
import jax
import jax.numpy as jnp
from jax import lax
from jax.sharding import PartitionSpec as P
from jax.experimental import pallas as pl
from jax.experimental.pallas import tpu as pltpu

BASELINE_CELSIUS = 15.0
LOG_BASE_Q = 0.6931471805599453
PRIOR_VAR = 0.09


def ground_efflux_forward(
    ground_warmth_celsius,
    wetness_factor,
    carbon_reservoirs,
    location_category,
    category_sensitivity_effect,
    reservoir_decay_effect,
):
    nclass = category_sensitivity_effect.shape[0]
    category_onehot = (
        location_category[None, :] == jnp.arange(nclass, dtype=jnp.int32)[:, None]
    ).astype(jnp.float32)
    log_q = (
        LOG_BASE_Q
        + jnp.dot(
            category_sensitivity_effect[None, :], category_onehot, precision=lax.Precision.HIGHEST
        )[0]
    )
    base = jnp.array([0.6, 0.25, 0.1], dtype=jnp.float32)
    rates = base[:, None] * jnp.exp(
        jnp.dot(reservoir_decay_effect, category_onehot, precision=lax.Precision.HIGHEST)
    )
    decay_lifetime = (ground_warmth_celsius - BASELINE_CELSIUS) / 10.0
    modifier = jnp.exp(log_q[None, :] * decay_lifetime) * wetness_factor
    device_number = (rates * carbon_reservoirs)[:, None, :] * modifier[None]
    return (category_onehot, decay_lifetime, device_number)


def _fields_kernel(cse_ref, rde_ref, cat_ref, warm_ref, wet_ref, carbon_ref, out_ref):
    nclass = cse_ref.shape[0]
    cat = cat_ref[...]
    picked_q = jnp.zeros(cat.shape, jnp.float32)
    picked = [jnp.zeros(cat.shape, jnp.float32) for _ in range(3)]
    for c in range(nclass):
        hit = cat == c
        picked_q = jnp.where(hit, cse_ref[c], picked_q)
        for p in range(3):
            picked[p] = jnp.where(hit, rde_ref[p, c], picked[p])
    log_q = LOG_BASE_Q + picked_q
    base = (0.6, 0.25, 0.1)
    held = [base[p] * jnp.exp(picked[p]) * carbon_ref[p : p + 1, :] for p in range(3)]
    category = cat.astype(jnp.float32)
    for t in range(warm_ref.shape[0]):
        tau = (warm_ref[t : t + 1, :] - BASELINE_CELSIUS) / 10.0
        modifier = jnp.exp(log_q * tau) * wet_ref[t : t + 1, :]
        parts = [held[p] * modifier for p in range(3)]
        flux = parts[0] + parts[1] + parts[2]
        fields = (
            flux.astype(jnp.bfloat16).astype(jnp.float32),
            flux * tau,
            parts[0],
            parts[1],
            parts[2],
            category,
        )
        for q, value in enumerate(fields):
            out_ref[q, t : t + 1, :] = value


def owner_fields(
    ground_warmth_celsius,
    wetness_factor,
    carbon_reservoirs,
    location_category,
    category_sensitivity_effect,
    reservoir_decay_effect,
):
    epochs, cells = ground_warmth_celsius.shape
    smem = pl.BlockSpec(memory_space=pltpu.SMEM)
    vmem = pl.BlockSpec(memory_space=pltpu.VMEM)
    return pl.pallas_call(
        _fields_kernel,
        out_shape=jax.ShapeDtypeStruct((6, epochs, cells), jnp.float32),
        in_specs=[smem, smem, vmem, vmem, vmem, vmem],
        out_specs=vmem,
    )(
        category_sensitivity_effect,
        reservoir_decay_effect,
        location_category.reshape(1, cells),
        ground_warmth_celsius,
        wetness_factor,
        carbon_reservoirs,
    )


def shards(
    sensitivity_blocks,
    block_placement_table,
    needed_tile_lists,
    location_category,
    ground_warmth_celsius,
    wetness_factor,
    carbon_reservoirs,
    category_sensitivity_effect,
    reservoir_decay_effect,
    measured_anomaly,
    retrieval_precision,
):
    tile = sensitivity_blocks.shape[1]
    epochs_each_device, locations_each_device = ground_warmth_celsius.shape
    tiles_dev = locations_each_device // tile
    local_ids = epochs_each_device * tiles_dev
    n_snd = lax.axis_size("snd")
    n_map = lax.axis_size("map")
    cap = needed_tile_lists.shape[1]
    rows_own = measured_anomaly.shape[0]
    rows_dev = rows_own * n_map
    lanes = jnp.pad(needed_tile_lists, ((0, 0), (0, tile - cap)))[:, None, :]
    requests = lax.all_to_all(lanes, "snd", 0, 0)[:, 0, :cap]
    live = requests >= 0
    nclass = category_sensitivity_effect.shape[0]
    own_fields = owner_fields(
        ground_warmth_celsius,
        wetness_factor,
        carbon_reservoirs,
        location_category,
        category_sensitivity_effect,
        reservoir_decay_effect,
    ).reshape(6, local_ids, tile)
    asked = (
        requests.reshape(-1)[:, None] == jnp.arange(local_ids, dtype=jnp.int32)[None, :]
    ).astype(jnp.float32)
    answer = jnp.einsum("rl,qlc->rqc", asked, own_fields, precision=lax.Precision.HIGHEST)
    answer, block_placement_table, needed_tile_lists = lax.optimization_barrier(
        (answer, block_placement_table, needed_tile_lists)
    )
    received = lax.all_to_all(answer.reshape(n_snd, cap * 6, tile), "snd", 0, 0).reshape(
        n_snd * cap, 6, tile
    )

    block_row = block_placement_table[0]
    block_tile = block_placement_table[1]
    block_slot = block_placement_table[2]
    owner = block_slot // epochs_each_device
    wanted = (block_slot % epochs_each_device) * tiles_dev + block_tile
    listed = needed_tile_lists.at[owner].get(mode="promise_in_bounds")
    within = jnp.argmax(listed == wanted[:, None], axis=1).astype(jnp.int32)
    position = owner * cap + within
    vectors = received[:, 0].at[position].get(mode="promise_in_bounds")
    vectors = vectors.astype(jnp.bfloat16)
    contrib = jnp.einsum(
        "bij,bj->bi", sensitivity_blocks, vectors, preferred_element_type=jnp.float32
    )
    row_hot = (jnp.arange(rows_dev, dtype=jnp.int32)[:, None] == block_row[None, :]).astype(
        jnp.float32
    )
    partial_rows = jnp.dot(row_hot, contrib, precision=lax.Precision.HIGHEST)

    me_map = lax.axis_index("map")
    first = me_map * rows_own
    payload = jnp.concatenate([partial_rows, measured_anomaly, retrieval_precision], axis=0)
    swapped = lax.all_to_all(
        jnp.broadcast_to(payload[None], (n_map,) + payload.shape), "map", 0, 0
    )
    model_rows = jnp.sum(swapped[:, :rows_dev], axis=0)
    anomaly_rows = swapped[:, rows_dev : rows_dev + rows_own].reshape(rows_dev, tile)
    precision_rows = swapped[:, rows_dev + rows_own :].reshape(rows_dev, tile)
    weighted_rows = ((model_rows - anomaly_rows) * precision_rows).astype(jnp.bfloat16)
    model_xco2 = lax.dynamic_slice(model_rows, (first, 0), (rows_own, tile))
    diff = model_xco2 - measured_anomaly
    misfit = 0.5 * jnp.sum(retrieval_precision * diff * diff)

    back_rows = weighted_rows.at[block_row].get(mode="promise_in_bounds")
    block_grads = jnp.einsum(
        "bij,bi->bj", sensitivity_blocks, back_rows, preferred_element_type=jnp.float32
    )
    outgoing = jax.ops.segment_sum(
        block_grads, position, num_segments=n_snd * cap, mode="promise_in_bounds"
    )

    class_hot = (
        received[:, 5][:, :, None] == jnp.arange(nclass, dtype=jnp.float32)[None, None, :]
    ).astype(jnp.float32)
    weighted_fields = outgoing[:, None, :] * received[:, 1:5]
    class_part = jnp.einsum(
        "pqc,pck->qk", weighted_fields, class_hot, precision=lax.Precision.HIGHEST
    )
    mine = jnp.concatenate([class_part.reshape(-1), misfit[None]])
    width = mine.shape[0]
    mine = jnp.pad(mine, (0, tile - width))
    parcel = jnp.concatenate(
        [
            outgoing.reshape(n_snd, cap, tile),
            jnp.broadcast_to(mine[None, None], (n_snd, 1, tile)),
        ],
        axis=1,
    )
    incoming = lax.all_to_all(parcel, "snd", 0, 0)
    column = jnp.sum(incoming[:, cap], axis=0)
    gathered = lax.all_to_all(jnp.broadcast_to(column[None], (n_map, tile)), "map", 0, 0)
    totals = jnp.sum(gathered, axis=0)[:width]

    target = jnp.where(live, requests, local_ids).reshape(-1)
    grad_tiles = jax.ops.segment_sum(
        incoming[:, :cap].reshape(n_snd * cap, tile),
        target,
        num_segments=local_ids + 1,
        mode="promise_in_bounds",
    )[:local_ids]
    flux_grad = grad_tiles.reshape(epochs_each_device, locations_each_device)

    class_total = totals[:-1].reshape(4, nclass)
    total_misfit = totals[-1]
    prior = (
        jnp.concatenate([category_sensitivity_effect[None, :], reservoir_decay_effect], axis=0)
        / PRIOR_VAR
    )
    class_grad = class_total + prior
    cost = (
        total_misfit
        + 0.5 * jnp.sum(category_sensitivity_effect * category_sensitivity_effect) / PRIOR_VAR
        + 0.5 * jnp.sum(reservoir_decay_effect * reservoir_decay_effect) / PRIOR_VAR
    )
    return (model_xco2, flux_grad, class_grad, cost)


def solution(mesh):
    in_specs = (
        P(("snd", "map"), None, None),
        P(None, ("snd", "map")),
        P(("snd", "map"), None),
        P("map"),
        P("snd", "map"),
        P("snd", "map"),
        P(None, "map"),
        P(),
        P(),
        P(("snd", "map"), None),
        P(("snd", "map"), None),
    )
    out_specs = (P(("snd", "map"), None), P("snd", "map"), P(), P())
    return jax.shard_map(shards, mesh=mesh, in_specs=in_specs, out_specs=out_specs, check_vma=False)
```

```python
import jax
import jax.numpy as jnp
from jax import lax
from jax.sharding import PartitionSpec as P
from jax.experimental import pallas as pl
from jax.experimental.pallas import tpu as pltpu

BASELINE_CELSIUS = 15.0
LOG_BASE_Q = 0.6931471805599453
PRIOR_VAR = 0.09


def ground_efflux_forward(
    ground_warmth_celsius,
    wetness_factor,
    carbon_reservoirs,
    location_category,
    category_sensitivity_effect,
    reservoir_decay_effect,
):
    nclass = category_sensitivity_effect.shape[0]
    category_onehot = (
        location_category[None, :] == jnp.arange(nclass, dtype=jnp.int32)[:, None]
    ).astype(jnp.float32)
    log_q = (
        LOG_BASE_Q
        + jnp.dot(
            category_sensitivity_effect[None, :], category_onehot, precision=lax.Precision.HIGHEST
        )[0]
    )
    base = jnp.array([0.6, 0.25, 0.1], dtype=jnp.float32)
    rates = base[:, None] * jnp.exp(
        jnp.dot(reservoir_decay_effect, category_onehot, precision=lax.Precision.HIGHEST)
    )
    decay_lifetime = (ground_warmth_celsius - BASELINE_CELSIUS) / 10.0
    modifier = jnp.exp(log_q[None, :] * decay_lifetime) * wetness_factor
    device_number = (rates * carbon_reservoirs)[:, None, :] * modifier[None]
    return (category_onehot, decay_lifetime, device_number)


def _fields_kernel(cse_ref, rde_ref, cat_ref, warm_ref, wet_ref, carbon_ref, out_ref):
    nclass = cse_ref.shape[0]
    cat = cat_ref[...]
    picked_q = jnp.zeros(cat.shape, jnp.float32)
    picked = [jnp.zeros(cat.shape, jnp.float32) for _ in range(3)]
    for c in range(nclass):
        hit = cat == c
        picked_q = jnp.where(hit, cse_ref[c], picked_q)
        for p in range(3):
            picked[p] = jnp.where(hit, rde_ref[p, c], picked[p])
    log_q = LOG_BASE_Q + picked_q
    base = (0.6, 0.25, 0.1)
    held = [base[p] * jnp.exp(picked[p]) * carbon_ref[p : p + 1, :] for p in range(3)]
    category = cat.astype(jnp.float32)
    for t in range(warm_ref.shape[0]):
        tau = (warm_ref[t : t + 1, :] - BASELINE_CELSIUS) / 10.0
        modifier = jnp.exp(log_q * tau) * wet_ref[t : t + 1, :]
        parts = [held[p] * modifier for p in range(3)]
        flux = parts[0] + parts[1] + parts[2]
        fields = (
            flux.astype(jnp.bfloat16).astype(jnp.float32),
            flux * tau,
            parts[0],
            parts[1],
            parts[2],
            category,
        )
        for q, value in enumerate(fields):
            out_ref[q, t : t + 1, :] = value


def owner_fields(
    ground_warmth_celsius,
    wetness_factor,
    carbon_reservoirs,
    location_category,
    category_sensitivity_effect,
    reservoir_decay_effect,
):
    epochs, cells = ground_warmth_celsius.shape
    smem = pl.BlockSpec(memory_space=pltpu.SMEM)
    vmem = pl.BlockSpec(memory_space=pltpu.VMEM)
    return pl.pallas_call(
        _fields_kernel,
        out_shape=jax.ShapeDtypeStruct((6, epochs, cells), jnp.float32),
        in_specs=[smem, smem, vmem, vmem, vmem, vmem],
        out_specs=vmem,
    )(
        category_sensitivity_effect,
        reservoir_decay_effect,
        location_category.reshape(1, cells),
        ground_warmth_celsius,
        wetness_factor,
        carbon_reservoirs,
    )


def shards(
    sensitivity_blocks,
    block_placement_table,
    needed_tile_lists,
    location_category,
    ground_warmth_celsius,
    wetness_factor,
    carbon_reservoirs,
    category_sensitivity_effect,
    reservoir_decay_effect,
    measured_anomaly,
    retrieval_precision,
):
    tile = sensitivity_blocks.shape[1]
    epochs_each_device, locations_each_device = ground_warmth_celsius.shape
    tiles_dev = locations_each_device // tile
    local_ids = epochs_each_device * tiles_dev
    n_snd = lax.axis_size("snd")
    n_map = lax.axis_size("map")
    cap = needed_tile_lists.shape[1]
    rows_own = measured_anomaly.shape[0]
    rows_dev = rows_own * n_map
    lanes = jnp.pad(needed_tile_lists, ((0, 0), (0, tile - cap)))[:, None, :]
    requests = lax.all_to_all(lanes, "snd", 0, 0)[:, 0, :cap]
    live = requests >= 0
    nclass = category_sensitivity_effect.shape[0]
    own_fields = owner_fields(
        ground_warmth_celsius,
        wetness_factor,
        carbon_reservoirs,
        location_category,
        category_sensitivity_effect,
        reservoir_decay_effect,
    ).reshape(6, local_ids, tile)
    own_fields, block_placement_table, needed_tile_lists = lax.optimization_barrier(
        (own_fields, block_placement_table, needed_tile_lists)
    )
    asked = (
        requests.reshape(-1)[:, None] == jnp.arange(local_ids, dtype=jnp.int32)[None, :]
    ).astype(jnp.float32)
    answer = jnp.einsum("rl,qlc->rqc", asked, own_fields, precision=lax.Precision.HIGHEST)
    received = lax.all_to_all(answer.reshape(n_snd, cap * 6, tile), "snd", 0, 0).reshape(
        n_snd * cap, 6, tile
    )

    block_row = block_placement_table[0]
    block_tile = block_placement_table[1]
    block_slot = block_placement_table[2]
    owner = block_slot // epochs_each_device
    wanted = (block_slot % epochs_each_device) * tiles_dev + block_tile
    listed = needed_tile_lists.at[owner].get(mode="promise_in_bounds")
    within = jnp.argmax(listed == wanted[:, None], axis=1).astype(jnp.int32)
    position = owner * cap + within
    vectors = received[:, 0].at[position].get(mode="promise_in_bounds")
    vectors = vectors.astype(jnp.bfloat16)
    contrib = jnp.einsum(
        "bij,bj->bi", sensitivity_blocks, vectors, preferred_element_type=jnp.float32
    )
    row_hot = (jnp.arange(rows_dev, dtype=jnp.int32)[:, None] == block_row[None, :]).astype(
        jnp.float32
    )
    partial_rows = jnp.dot(row_hot, contrib, precision=lax.Precision.HIGHEST)

    me_map = lax.axis_index("map")
    first = me_map * rows_own
    payload = jnp.concatenate([partial_rows, measured_anomaly, retrieval_precision], axis=0)
    swapped = lax.all_to_all(
        jnp.broadcast_to(payload[None], (n_map,) + payload.shape), "map", 0, 0
    )
    model_rows = jnp.sum(swapped[:, :rows_dev], axis=0)
    anomaly_rows = swapped[:, rows_dev : rows_dev + rows_own].reshape(rows_dev, tile)
    precision_rows = swapped[:, rows_dev + rows_own :].reshape(rows_dev, tile)
    weighted_rows = ((model_rows - anomaly_rows) * precision_rows).astype(jnp.bfloat16)
    model_xco2 = lax.dynamic_slice(model_rows, (first, 0), (rows_own, tile))
    diff = model_xco2 - measured_anomaly
    misfit = 0.5 * jnp.sum(retrieval_precision * diff * diff)

    back_rows = weighted_rows.at[block_row].get(mode="promise_in_bounds")
    block_grads = jnp.einsum(
        "bij,bi->bj", sensitivity_blocks, back_rows, preferred_element_type=jnp.float32
    )
    outgoing = jax.ops.segment_sum(
        block_grads, position, num_segments=n_snd * cap, mode="promise_in_bounds"
    )

    class_hot = (
        received[:, 5][:, :, None] == jnp.arange(nclass, dtype=jnp.float32)[None, None, :]
    ).astype(jnp.float32)
    weighted_fields = outgoing[:, None, :] * received[:, 1:5]
    class_part = jnp.einsum(
        "pqc,pck->qk", weighted_fields, class_hot, precision=lax.Precision.HIGHEST
    )
    mine = jnp.concatenate([class_part.reshape(-1), misfit[None]])
    width = mine.shape[0]
    mine = jnp.pad(mine, (0, tile - width))
    parcel = jnp.concatenate(
        [
            outgoing.reshape(n_snd, cap, tile),
            jnp.broadcast_to(mine[None, None], (n_snd, 1, tile)),
        ],
        axis=1,
    )
    incoming = lax.all_to_all(parcel, "snd", 0, 0)
    column = jnp.sum(incoming[:, cap], axis=0)
    gathered = lax.all_to_all(jnp.broadcast_to(column[None], (n_map, tile)), "map", 0, 0)
    totals = jnp.sum(gathered, axis=0)[:width]

    target = jnp.where(live, requests, local_ids).reshape(-1)
    grad_tiles = jax.ops.segment_sum(
        incoming[:, :cap].reshape(n_snd * cap, tile),
        target,
        num_segments=local_ids + 1,
        mode="promise_in_bounds",
    )[:local_ids]
    flux_grad = grad_tiles.reshape(epochs_each_device, locations_each_device)

    class_total = totals[:-1].reshape(4, nclass)
    total_misfit = totals[-1]
    prior = (
        jnp.concatenate([category_sensitivity_effect[None, :], reservoir_decay_effect], axis=0)
        / PRIOR_VAR
    )
    class_grad = class_total + prior
    cost = (
        total_misfit
        + 0.5 * jnp.sum(category_sensitivity_effect * category_sensitivity_effect) / PRIOR_VAR
        + 0.5 * jnp.sum(reservoir_decay_effect * reservoir_decay_effect) / PRIOR_VAR
    )
    return (model_xco2, flux_grad, class_grad, cost)


def solution(mesh):
    in_specs = (
        P(("snd", "map"), None, None),
        P(None, ("snd", "map")),
        P(("snd", "map"), None),
        P("map"),
        P("snd", "map"),
        P("snd", "map"),
        P(None, "map"),
        P(),
        P(),
        P(("snd", "map"), None),
        P(("snd", "map"), None),
    )
    out_specs = (P(("snd", "map"), None), P("snd", "map"), P(), P())
    return jax.shard_map(shards, mesh=mesh, in_specs=in_specs, out_specs=out_specs, check_vma=False)
```

```python
import jax
import jax.numpy as jnp
from jax import lax
from jax.sharding import PartitionSpec as P
from jax.experimental import pallas as pl
from jax.experimental.pallas import tpu as pltpu

BASELINE_CELSIUS = 15.0
LOG_BASE_Q = 0.6931471805599453
PRIOR_VAR = 0.09


def ground_efflux_forward(
    ground_warmth_celsius,
    wetness_factor,
    carbon_reservoirs,
    location_category,
    category_sensitivity_effect,
    reservoir_decay_effect,
):
    nclass = category_sensitivity_effect.shape[0]
    category_onehot = (
        location_category[None, :] == jnp.arange(nclass, dtype=jnp.int32)[:, None]
    ).astype(jnp.float32)
    log_q = (
        LOG_BASE_Q
        + jnp.dot(
            category_sensitivity_effect[None, :], category_onehot, precision=lax.Precision.HIGHEST
        )[0]
    )
    base = jnp.array([0.6, 0.25, 0.1], dtype=jnp.float32)
    rates = base[:, None] * jnp.exp(
        jnp.dot(reservoir_decay_effect, category_onehot, precision=lax.Precision.HIGHEST)
    )
    decay_lifetime = (ground_warmth_celsius - BASELINE_CELSIUS) / 10.0
    modifier = jnp.exp(log_q[None, :] * decay_lifetime) * wetness_factor
    device_number = (rates * carbon_reservoirs)[:, None, :] * modifier[None]
    return (category_onehot, decay_lifetime, device_number)


def _fields_kernel(cse_ref, rde_ref, cat_ref, warm_ref, wet_ref, carbon_ref, out_ref):
    nclass = cse_ref.shape[0]
    cat = cat_ref[...]
    picked_q = jnp.zeros(cat.shape, jnp.float32)
    picked = [jnp.zeros(cat.shape, jnp.float32) for _ in range(3)]
    for c in range(nclass):
        hit = cat == c
        picked_q = jnp.where(hit, cse_ref[c], picked_q)
        for p in range(3):
            picked[p] = jnp.where(hit, rde_ref[p, c], picked[p])
    log_q = LOG_BASE_Q + picked_q
    base = (0.6, 0.25, 0.1)
    held = [base[p] * jnp.exp(picked[p]) * carbon_ref[p : p + 1, :] for p in range(3)]
    category = cat.astype(jnp.float32)
    for t in range(warm_ref.shape[0]):
        tau = (warm_ref[t : t + 1, :] - BASELINE_CELSIUS) / 10.0
        modifier = jnp.exp(log_q * tau) * wet_ref[t : t + 1, :]
        parts = [held[p] * modifier for p in range(3)]
        flux = parts[0] + parts[1] + parts[2]
        fields = (
            flux.astype(jnp.bfloat16).astype(jnp.float32),
            flux * tau,
            parts[0],
            parts[1],
            parts[2],
            category,
        )
        for q, value in enumerate(fields):
            out_ref[q, t : t + 1, :] = value


def owner_fields(
    ground_warmth_celsius,
    wetness_factor,
    carbon_reservoirs,
    location_category,
    category_sensitivity_effect,
    reservoir_decay_effect,
):
    epochs, cells = ground_warmth_celsius.shape
    smem = pl.BlockSpec(memory_space=pltpu.SMEM)
    vmem = pl.BlockSpec(memory_space=pltpu.VMEM)
    return pl.pallas_call(
        _fields_kernel,
        out_shape=jax.ShapeDtypeStruct((6, epochs, cells), jnp.float32),
        in_specs=[smem, smem, vmem, vmem, vmem, vmem],
        out_specs=vmem,
    )(
        category_sensitivity_effect,
        reservoir_decay_effect,
        location_category.reshape(1, cells),
        ground_warmth_celsius,
        wetness_factor,
        carbon_reservoirs,
    )


def shards(
    sensitivity_blocks,
    block_placement_table,
    needed_tile_lists,
    location_category,
    ground_warmth_celsius,
    wetness_factor,
    carbon_reservoirs,
    category_sensitivity_effect,
    reservoir_decay_effect,
    measured_anomaly,
    retrieval_precision,
):
    tile = sensitivity_blocks.shape[1]
    epochs_each_device, locations_each_device = ground_warmth_celsius.shape
    tiles_dev = locations_each_device // tile
    local_ids = epochs_each_device * tiles_dev
    n_snd = lax.axis_size("snd")
    n_map = lax.axis_size("map")
    cap = needed_tile_lists.shape[1]
    rows_own = measured_anomaly.shape[0]
    rows_dev = rows_own * n_map
    lanes = jnp.pad(needed_tile_lists, ((0, 0), (0, tile - cap)))[:, None, :]
    requests = lax.all_to_all(lanes, "snd", 0, 0)[:, 0, :cap]
    live = requests >= 0
    nclass = category_sensitivity_effect.shape[0]
    own_fields = owner_fields(
        ground_warmth_celsius,
        wetness_factor,
        carbon_reservoirs,
        location_category,
        category_sensitivity_effect,
        reservoir_decay_effect,
    ).reshape(6, local_ids, tile)
    own_fields, block_placement_table, needed_tile_lists = lax.optimization_barrier(
        (own_fields, block_placement_table, needed_tile_lists)
    )
    asked = (
        requests.reshape(-1)[:, None] == jnp.arange(local_ids, dtype=jnp.int32)[None, :]
    ).astype(jnp.float32)
    answer = jnp.einsum("rl,qlc->rqc", asked, own_fields, precision=lax.Precision.HIGHEST)
    received = lax.all_to_all(answer.reshape(n_snd, cap * 6, tile), "snd", 0, 0).reshape(
        n_snd * cap, 6, tile
    )

    block_row = block_placement_table[0]
    block_tile = block_placement_table[1]
    block_slot = block_placement_table[2]
    owner = block_slot // epochs_each_device
    wanted = (block_slot % epochs_each_device) * tiles_dev + block_tile
    listed = needed_tile_lists.at[owner].get(mode="promise_in_bounds")
    within = jnp.argmax(listed == wanted[:, None], axis=1).astype(jnp.int32)
    position = owner * cap + within
    vectors = received[:, 0].at[position].get(mode="promise_in_bounds")
    vectors = vectors.astype(jnp.bfloat16)
    contrib = jnp.einsum(
        "bij,bj->bi", sensitivity_blocks, vectors, preferred_element_type=jnp.float32
    )
    row_hot = (jnp.arange(rows_dev, dtype=jnp.int32)[:, None] == block_row[None, :]).astype(
        jnp.float32
    )
    partial_rows = jnp.dot(row_hot, contrib, precision=lax.Precision.HIGHEST)

    me_map = lax.axis_index("map")
    first = me_map * rows_own
    payload = jnp.concatenate([partial_rows, measured_anomaly, retrieval_precision], axis=0)
    swapped = lax.all_to_all(
        jnp.broadcast_to(payload[None], (n_map,) + payload.shape), "map", 0, 0
    )
    model_rows = jnp.sum(swapped[:, :rows_dev], axis=0)
    anomaly_rows = swapped[:, rows_dev : rows_dev + rows_own].reshape(rows_dev, tile)
    precision_rows = swapped[:, rows_dev + rows_own :].reshape(rows_dev, tile)
    diff_rows = model_rows - anomaly_rows
    weighted_rows = (diff_rows * precision_rows).astype(jnp.bfloat16)
    model_xco2 = lax.dynamic_slice(model_rows, (first, 0), (rows_own, tile))
    shard_misfit = 0.5 * jnp.sum(precision_rows * diff_rows * diff_rows)
    misfit = jnp.where(me_map == 0, shard_misfit, 0.0)

    back_rows = weighted_rows.at[block_row].get(mode="promise_in_bounds")
    block_grads = jnp.einsum(
        "bij,bi->bj", sensitivity_blocks, back_rows, preferred_element_type=jnp.float32
    )
    outgoing = jax.ops.segment_sum(
        block_grads, position, num_segments=n_snd * cap, mode="promise_in_bounds"
    )

    class_hot = (
        received[:, 5][:, :, None] == jnp.arange(nclass, dtype=jnp.float32)[None, None, :]
    ).astype(jnp.float32)
    weighted_fields = outgoing[:, None, :] * received[:, 1:5]
    class_part = jnp.einsum(
        "pqc,pck->qk", weighted_fields, class_hot, precision=lax.Precision.HIGHEST
    )
    mine = jnp.concatenate([class_part.reshape(-1), misfit[None]])
    width = mine.shape[0]
    mine = jnp.pad(mine, (0, tile - width))
    parcel = jnp.concatenate(
        [
            outgoing.reshape(n_snd, cap, tile),
            jnp.broadcast_to(mine[None, None], (n_snd, 1, tile)),
        ],
        axis=1,
    )
    incoming = lax.all_to_all(parcel, "snd", 0, 0)
    column = jnp.sum(incoming[:, cap], axis=0)
    gathered = lax.all_to_all(jnp.broadcast_to(column[None], (n_map, tile)), "map", 0, 0)
    totals = jnp.sum(gathered, axis=0)[:width]

    target = jnp.where(live, requests, local_ids).reshape(-1)
    grad_tiles = jax.ops.segment_sum(
        incoming[:, :cap].reshape(n_snd * cap, tile),
        target,
        num_segments=local_ids + 1,
        mode="promise_in_bounds",
    )[:local_ids]
    flux_grad = grad_tiles.reshape(epochs_each_device, locations_each_device)

    class_total = totals[:-1].reshape(4, nclass)
    total_misfit = totals[-1]
    prior = (
        jnp.concatenate([category_sensitivity_effect[None, :], reservoir_decay_effect], axis=0)
        / PRIOR_VAR
    )
    class_grad = class_total + prior
    cost = (
        total_misfit
        + 0.5 * jnp.sum(category_sensitivity_effect * category_sensitivity_effect) / PRIOR_VAR
        + 0.5 * jnp.sum(reservoir_decay_effect * reservoir_decay_effect) / PRIOR_VAR
    )
    return (model_xco2, flux_grad, class_grad, cost)


def solution(mesh):
    in_specs = (
        P(("snd", "map"), None, None),
        P(None, ("snd", "map")),
        P(("snd", "map"), None),
        P("map"),
        P("snd", "map"),
        P("snd", "map"),
        P(None, "map"),
        P(),
        P(),
        P(("snd", "map"), None),
        P(("snd", "map"), None),
    )
    out_specs = (P(("snd", "map"), None), P("snd", "map"), P(), P())
    return jax.shard_map(shards, mesh=mesh, in_specs=in_specs, out_specs=out_specs, check_vma=False)
```

```python
import jax
import jax.numpy as jnp
from jax import lax
from jax.sharding import PartitionSpec as P
from jax.experimental import pallas as pl
from jax.experimental.pallas import tpu as pltpu

BASELINE_CELSIUS = 15.0
LOG_BASE_Q = 0.6931471805599453
PRIOR_VAR = 0.09


def ground_efflux_forward(
    ground_warmth_celsius,
    wetness_factor,
    carbon_reservoirs,
    location_category,
    category_sensitivity_effect,
    reservoir_decay_effect,
):
    nclass = category_sensitivity_effect.shape[0]
    category_onehot = (
        location_category[None, :] == jnp.arange(nclass, dtype=jnp.int32)[:, None]
    ).astype(jnp.float32)
    log_q = (
        LOG_BASE_Q
        + jnp.dot(
            category_sensitivity_effect[None, :], category_onehot, precision=lax.Precision.HIGHEST
        )[0]
    )
    base = jnp.array([0.6, 0.25, 0.1], dtype=jnp.float32)
    rates = base[:, None] * jnp.exp(
        jnp.dot(reservoir_decay_effect, category_onehot, precision=lax.Precision.HIGHEST)
    )
    decay_lifetime = (ground_warmth_celsius - BASELINE_CELSIUS) / 10.0
    modifier = jnp.exp(log_q[None, :] * decay_lifetime) * wetness_factor
    device_number = (rates * carbon_reservoirs)[:, None, :] * modifier[None]
    return (category_onehot, decay_lifetime, device_number)


def _fields_kernel(cse_ref, rde_ref, cat_ref, warm_ref, wet_ref, carbon_ref, out_ref):
    nclass = cse_ref.shape[0]
    cat = cat_ref[...]
    picked_q = jnp.zeros(cat.shape, jnp.float32)
    picked = [jnp.zeros(cat.shape, jnp.float32) for _ in range(3)]
    for c in range(nclass):
        hit = cat == c
        picked_q = jnp.where(hit, cse_ref[c], picked_q)
        for p in range(3):
            picked[p] = jnp.where(hit, rde_ref[p, c], picked[p])
    log_q = LOG_BASE_Q + picked_q
    base = (0.6, 0.25, 0.1)
    held = [base[p] * jnp.exp(picked[p]) * carbon_ref[p : p + 1, :] for p in range(3)]
    category = cat.astype(jnp.float32)
    for t in range(warm_ref.shape[0]):
        tau = (warm_ref[t : t + 1, :] - BASELINE_CELSIUS) / 10.0
        modifier = jnp.exp(log_q * tau) * wet_ref[t : t + 1, :]
        parts = [held[p] * modifier for p in range(3)]
        flux = parts[0] + parts[1] + parts[2]
        fields = (
            flux.astype(jnp.bfloat16).astype(jnp.float32),
            flux * tau,
            parts[0],
            parts[1],
            parts[2],
            category,
        )
        for q, value in enumerate(fields):
            out_ref[q, t : t + 1, :] = value


def owner_fields(
    ground_warmth_celsius,
    wetness_factor,
    carbon_reservoirs,
    location_category,
    category_sensitivity_effect,
    reservoir_decay_effect,
):
    epochs, cells = ground_warmth_celsius.shape
    smem = pl.BlockSpec(memory_space=pltpu.SMEM)
    vmem = pl.BlockSpec(memory_space=pltpu.VMEM)
    return pl.pallas_call(
        _fields_kernel,
        out_shape=jax.ShapeDtypeStruct((6, epochs, cells), jnp.float32),
        in_specs=[smem, smem, vmem, vmem, vmem, vmem],
        out_specs=vmem,
    )(
        category_sensitivity_effect,
        reservoir_decay_effect,
        location_category.reshape(1, cells),
        ground_warmth_celsius,
        wetness_factor,
        carbon_reservoirs,
    )


def shards(
    sensitivity_blocks,
    block_placement_table,
    needed_tile_lists,
    location_category,
    ground_warmth_celsius,
    wetness_factor,
    carbon_reservoirs,
    category_sensitivity_effect,
    reservoir_decay_effect,
    measured_anomaly,
    retrieval_precision,
):
    tile = sensitivity_blocks.shape[1]
    epochs_each_device, locations_each_device = ground_warmth_celsius.shape
    tiles_dev = locations_each_device // tile
    local_ids = epochs_each_device * tiles_dev
    n_snd = lax.axis_size("snd")
    n_map = lax.axis_size("map")
    cap = needed_tile_lists.shape[1]
    rows_own = measured_anomaly.shape[0]
    rows_dev = rows_own * n_map
    lanes = jnp.pad(needed_tile_lists, ((0, 0), (0, tile - cap)))[:, None, :]
    requests = lax.all_to_all(lanes, "snd", 0, 0)[:, 0, :cap]
    live = requests >= 0
    nclass = category_sensitivity_effect.shape[0]
    own_fields = owner_fields(
        ground_warmth_celsius,
        wetness_factor,
        carbon_reservoirs,
        location_category,
        category_sensitivity_effect,
        reservoir_decay_effect,
    ).reshape(6, local_ids, tile)
    own_fields, block_placement_table, needed_tile_lists = lax.optimization_barrier(
        (own_fields, block_placement_table, needed_tile_lists)
    )
    asked = (
        requests.reshape(-1)[:, None] == jnp.arange(local_ids, dtype=jnp.int32)[None, :]
    ).astype(jnp.float32)
    answer = jnp.einsum("rl,qlc->rqc", asked, own_fields, precision=lax.Precision.HIGHEST)
    received = lax.all_to_all(answer.reshape(n_snd, cap * 6, tile), "snd", 0, 0).reshape(
        n_snd * cap, 6, tile
    )

    block_row = block_placement_table[0]
    block_tile = block_placement_table[1]
    block_slot = block_placement_table[2]
    owner = block_slot // epochs_each_device
    wanted = (block_slot % epochs_each_device) * tiles_dev + block_tile
    listed = needed_tile_lists.at[owner].get(mode="promise_in_bounds")
    within = jnp.argmax(listed == wanted[:, None], axis=1).astype(jnp.int32)
    position = owner * cap + within
    vectors = received[:, 0].at[position].get(mode="promise_in_bounds")
    vectors = vectors.astype(jnp.bfloat16)
    contrib = jnp.einsum(
        "bij,bj->bi", sensitivity_blocks, vectors, preferred_element_type=jnp.float32
    )
    row_hot = (jnp.arange(rows_dev, dtype=jnp.int32)[:, None] == block_row[None, :]).astype(
        jnp.float32
    )
    partial_rows = jnp.dot(row_hot, contrib, precision=lax.Precision.HIGHEST)

    me_map = lax.axis_index("map")
    first = me_map * rows_own
    payload = jnp.concatenate([partial_rows, measured_anomaly, retrieval_precision], axis=0)
    swapped = lax.all_to_all(
        jnp.broadcast_to(payload[None], (n_map,) + payload.shape), "map", 0, 0
    )
    model_rows = jnp.sum(swapped[:, :rows_dev], axis=0)
    anomaly_rows = swapped[:, rows_dev : rows_dev + rows_own].reshape(rows_dev, tile)
    precision_rows = swapped[:, rows_dev + rows_own :].reshape(rows_dev, tile)
    diff_rows = model_rows - anomaly_rows
    weighted_rows = (diff_rows * precision_rows).astype(jnp.bfloat16)
    model_xco2 = lax.dynamic_slice(model_rows, (first, 0), (rows_own, tile))
    shard_misfit = 0.5 * jnp.sum(precision_rows * diff_rows * diff_rows)
    misfit = jnp.where(me_map == 0, shard_misfit, 0.0)

    back_rows = weighted_rows.at[block_row].get(mode="promise_in_bounds")
    block_grads = jnp.einsum(
        "bij,bi->bj", sensitivity_blocks, back_rows, preferred_element_type=jnp.float32
    )
    outgoing = jax.ops.segment_sum(
        block_grads, position, num_segments=n_snd * cap, mode="promise_in_bounds"
    )

    class_hot = (
        received[:, 5][:, :, None] == jnp.arange(nclass, dtype=jnp.float32)[None, None, :]
    ).astype(jnp.float32)
    weighted_fields = outgoing[:, None, :] * received[:, 1:5]
    class_part = jnp.einsum(
        "pqc,pck->qk", weighted_fields, class_hot, precision=lax.Precision.HIGHEST
    )
    prior = (
        jnp.concatenate([category_sensitivity_effect[None, :], reservoir_decay_effect], axis=0)
        / PRIOR_VAR
    )
    prior_cost = (
        0.5 * jnp.sum(category_sensitivity_effect * category_sensitivity_effect) / PRIOR_VAR
        + 0.5 * jnp.sum(reservoir_decay_effect * reservoir_decay_effect) / PRIOR_VAR
    )
    first_device = (me_map == 0) & (lax.axis_index("snd") == 0)
    priors = jnp.where(first_device, jnp.concatenate([prior.reshape(-1), prior_cost[None]]), 0.0)
    mine = jnp.concatenate([class_part.reshape(-1), misfit[None]]) + priors
    width = mine.shape[0]
    mine = jnp.pad(mine, (0, tile - width))
    parcel = jnp.concatenate(
        [
            outgoing.reshape(n_snd, cap, tile),
            jnp.broadcast_to(mine[None, None], (n_snd, 1, tile)),
        ],
        axis=1,
    )
    incoming = lax.all_to_all(parcel, "snd", 0, 0)
    column = jnp.sum(incoming[:, cap], axis=0)
    gathered = lax.all_to_all(jnp.broadcast_to(column[None], (n_map, tile)), "map", 0, 0)
    totals = jnp.sum(gathered, axis=0)[:width]

    target = jnp.where(live, requests, local_ids).reshape(-1)
    grad_tiles = jax.ops.segment_sum(
        incoming[:, :cap].reshape(n_snd * cap, tile),
        target,
        num_segments=local_ids + 1,
        mode="promise_in_bounds",
    )[:local_ids]
    flux_grad = grad_tiles.reshape(epochs_each_device, locations_each_device)

    class_grad = totals[:-1].reshape(4, nclass)
    cost = totals[-1]
    return (model_xco2, flux_grad, class_grad, cost)


def solution(mesh):
    in_specs = (
        P(("snd", "map"), None, None),
        P(None, ("snd", "map")),
        P(("snd", "map"), None),
        P("map"),
        P("snd", "map"),
        P("snd", "map"),
        P(None, "map"),
        P(),
        P(),
        P(("snd", "map"), None),
        P(("snd", "map"), None),
    )
    out_specs = (P(("snd", "map"), None), P("snd", "map"), P(), P())
    return jax.shard_map(shards, mesh=mesh, in_specs=in_specs, out_specs=out_specs, check_vma=False)
```

```python
import jax
import jax.numpy as jnp
from jax import lax
from jax.sharding import PartitionSpec as P
from jax.experimental import pallas as pl
from jax.experimental.pallas import tpu as pltpu

BASELINE_CELSIUS = 15.0
LOG_BASE_Q = 0.6931471805599453
PRIOR_VAR = 0.09
FIELDS = 8


def ground_efflux_forward(
    ground_warmth_celsius,
    wetness_factor,
    carbon_reservoirs,
    location_category,
    category_sensitivity_effect,
    reservoir_decay_effect,
):
    nclass = category_sensitivity_effect.shape[0]
    category_onehot = (
        location_category[None, :] == jnp.arange(nclass, dtype=jnp.int32)[:, None]
    ).astype(jnp.float32)
    log_q = (
        LOG_BASE_Q
        + jnp.dot(
            category_sensitivity_effect[None, :], category_onehot, precision=lax.Precision.HIGHEST
        )[0]
    )
    base = jnp.array([0.6, 0.25, 0.1], dtype=jnp.float32)
    rates = base[:, None] * jnp.exp(
        jnp.dot(reservoir_decay_effect, category_onehot, precision=lax.Precision.HIGHEST)
    )
    decay_lifetime = (ground_warmth_celsius - BASELINE_CELSIUS) / 10.0
    modifier = jnp.exp(log_q[None, :] * decay_lifetime) * wetness_factor
    device_number = (rates * carbon_reservoirs)[:, None, :] * modifier[None]
    return (category_onehot, decay_lifetime, device_number)


def _fields_kernel(cse_ref, rde_ref, cat_ref, warm_ref, wet_ref, carbon_ref, out_ref):
    nclass = cse_ref.shape[0]
    cat = cat_ref[...]
    picked_q = jnp.zeros(cat.shape, jnp.float32)
    picked = [jnp.zeros(cat.shape, jnp.float32) for _ in range(3)]
    for c in range(nclass):
        hit = cat == c
        picked_q = jnp.where(hit, cse_ref[c], picked_q)
        for p in range(3):
            picked[p] = jnp.where(hit, rde_ref[p, c], picked[p])
    log_q = LOG_BASE_Q + picked_q
    base = (0.6, 0.25, 0.1)
    held = [base[p] * jnp.exp(picked[p]) * carbon_ref[p : p + 1, :] for p in range(3)]
    category = cat.astype(jnp.float32)
    for t in range(warm_ref.shape[0]):
        tau = (warm_ref[t : t + 1, :] - BASELINE_CELSIUS) / 10.0
        modifier = jnp.exp(log_q * tau) * wet_ref[t : t + 1, :]
        parts = [held[p] * modifier for p in range(3)]
        flux = parts[0] + parts[1] + parts[2]
        fields = (
            flux.astype(jnp.bfloat16).astype(jnp.float32),
            flux * tau,
            parts[0],
            parts[1],
            parts[2],
            category,
        )
        for q, value in enumerate(fields):
            out_ref[q, t : t + 1, :] = value
        for q in range(len(fields), out_ref.shape[0]):
            out_ref[q, t : t + 1, :] = jnp.zeros_like(category)


def owner_fields(
    ground_warmth_celsius,
    wetness_factor,
    carbon_reservoirs,
    location_category,
    category_sensitivity_effect,
    reservoir_decay_effect,
):
    epochs, cells = ground_warmth_celsius.shape
    smem = pl.BlockSpec(memory_space=pltpu.SMEM)
    vmem = pl.BlockSpec(memory_space=pltpu.VMEM)
    return pl.pallas_call(
        _fields_kernel,
        out_shape=jax.ShapeDtypeStruct((FIELDS, epochs, cells), jnp.float32),
        in_specs=[smem, smem, vmem, vmem, vmem, vmem],
        out_specs=vmem,
    )(
        category_sensitivity_effect,
        reservoir_decay_effect,
        location_category.reshape(1, cells),
        ground_warmth_celsius,
        wetness_factor,
        carbon_reservoirs,
    )


def shards(
    sensitivity_blocks,
    block_placement_table,
    needed_tile_lists,
    location_category,
    ground_warmth_celsius,
    wetness_factor,
    carbon_reservoirs,
    category_sensitivity_effect,
    reservoir_decay_effect,
    measured_anomaly,
    retrieval_precision,
):
    tile = sensitivity_blocks.shape[1]
    epochs_each_device, locations_each_device = ground_warmth_celsius.shape
    tiles_dev = locations_each_device // tile
    local_ids = epochs_each_device * tiles_dev
    n_snd = lax.axis_size("snd")
    n_map = lax.axis_size("map")
    cap = needed_tile_lists.shape[1]
    rows_own = measured_anomaly.shape[0]
    rows_dev = rows_own * n_map
    lanes = jnp.pad(needed_tile_lists, ((0, 0), (0, tile - cap)))[:, None, :]
    requests = lax.all_to_all(lanes, "snd", 0, 0)[:, 0, :cap]
    live = requests >= 0
    nclass = category_sensitivity_effect.shape[0]
    own_fields = owner_fields(
        ground_warmth_celsius,
        wetness_factor,
        carbon_reservoirs,
        location_category,
        category_sensitivity_effect,
        reservoir_decay_effect,
    ).reshape(FIELDS, local_ids, tile)
    own_fields, block_placement_table, needed_tile_lists = lax.optimization_barrier(
        (own_fields, block_placement_table, needed_tile_lists)
    )
    asked = (
        requests.reshape(-1)[:, None] == jnp.arange(local_ids, dtype=jnp.int32)[None, :]
    ).astype(jnp.float32)
    answer = jnp.einsum("rl,qlc->rqc", asked, own_fields, precision=lax.Precision.HIGHEST)
    received = lax.all_to_all(answer.reshape(n_snd, cap * FIELDS, tile), "snd", 0, 0).reshape(
        n_snd * cap, FIELDS, tile
    )

    block_row = block_placement_table[0]
    block_tile = block_placement_table[1]
    block_slot = block_placement_table[2]
    owner = block_slot // epochs_each_device
    wanted = (block_slot % epochs_each_device) * tiles_dev + block_tile
    listed = needed_tile_lists.at[owner].get(mode="promise_in_bounds")
    within = jnp.argmax(listed == wanted[:, None], axis=1).astype(jnp.int32)
    position = owner * cap + within
    vectors = received[:, 0].at[position].get(mode="promise_in_bounds")
    vectors = vectors.astype(jnp.bfloat16)
    contrib = jnp.einsum(
        "bij,bj->bi", sensitivity_blocks, vectors, preferred_element_type=jnp.float32
    )
    row_hot = (jnp.arange(rows_dev, dtype=jnp.int32)[:, None] == block_row[None, :]).astype(
        jnp.float32
    )
    partial_rows = jnp.dot(row_hot, contrib, precision=lax.Precision.HIGHEST)

    me_map = lax.axis_index("map")
    first = me_map * rows_own
    payload = jnp.concatenate([partial_rows, measured_anomaly, retrieval_precision], axis=0)
    swapped = lax.all_to_all(
        jnp.broadcast_to(payload[None], (n_map,) + payload.shape), "map", 0, 0
    )
    model_rows = jnp.sum(swapped[:, :rows_dev], axis=0)
    anomaly_rows = swapped[:, rows_dev : rows_dev + rows_own].reshape(rows_dev, tile)
    precision_rows = swapped[:, rows_dev + rows_own :].reshape(rows_dev, tile)
    diff_rows = model_rows - anomaly_rows
    weighted_rows = (diff_rows * precision_rows).astype(jnp.bfloat16)
    model_xco2 = lax.dynamic_slice(model_rows, (first, 0), (rows_own, tile))
    shard_misfit = 0.5 * jnp.sum(precision_rows * diff_rows * diff_rows)
    misfit = jnp.where(me_map == 0, shard_misfit, 0.0)

    back_rows = weighted_rows.at[block_row].get(mode="promise_in_bounds")
    block_grads = jnp.einsum(
        "bij,bi->bj", sensitivity_blocks, back_rows, preferred_element_type=jnp.float32
    )
    outgoing = jax.ops.segment_sum(
        block_grads, position, num_segments=n_snd * cap, mode="promise_in_bounds"
    )

    class_hot = (
        received[:, 5][:, :, None] == jnp.arange(nclass, dtype=jnp.float32)[None, None, :]
    ).astype(jnp.float32)
    weighted_fields = outgoing[:, None, :] * received[:, 1:5]
    class_part = jnp.einsum(
        "pqc,pck->qk", weighted_fields, class_hot, precision=lax.Precision.HIGHEST
    )
    prior = (
        jnp.concatenate([category_sensitivity_effect[None, :], reservoir_decay_effect], axis=0)
        / PRIOR_VAR
    )
    prior_cost = (
        0.5 * jnp.sum(category_sensitivity_effect * category_sensitivity_effect) / PRIOR_VAR
        + 0.5 * jnp.sum(reservoir_decay_effect * reservoir_decay_effect) / PRIOR_VAR
    )
    first_device = (me_map == 0) & (lax.axis_index("snd") == 0)
    priors = jnp.where(first_device, jnp.concatenate([prior.reshape(-1), prior_cost[None]]), 0.0)
    mine = jnp.concatenate([class_part.reshape(-1), misfit[None]]) + priors
    width = mine.shape[0]
    mine = jnp.pad(mine, (0, tile - width))
    parcel = jnp.concatenate(
        [
            outgoing.reshape(n_snd, cap, tile),
            jnp.broadcast_to(mine[None, None], (n_snd, 1, tile)),
        ],
        axis=1,
    )
    incoming = lax.all_to_all(parcel, "snd", 0, 0)
    column = jnp.sum(incoming[:, cap], axis=0)
    gathered = lax.all_to_all(jnp.broadcast_to(column[None], (n_map, tile)), "map", 0, 0)
    totals = jnp.sum(gathered, axis=0)[:width]

    target = jnp.where(live, requests, local_ids).reshape(-1)
    grad_tiles = jax.ops.segment_sum(
        incoming[:, :cap].reshape(n_snd * cap, tile),
        target,
        num_segments=local_ids + 1,
        mode="promise_in_bounds",
    )[:local_ids]
    flux_grad = grad_tiles.reshape(epochs_each_device, locations_each_device)

    class_grad = totals[:-1].reshape(4, nclass)
    cost = totals[-1]
    return (model_xco2, flux_grad, class_grad, cost)


def solution(mesh):
    in_specs = (
        P(("snd", "map"), None, None),
        P(None, ("snd", "map")),
        P(("snd", "map"), None),
        P("map"),
        P("snd", "map"),
        P("snd", "map"),
        P(None, "map"),
        P(),
        P(),
        P(("snd", "map"), None),
        P(("snd", "map"), None),
    )
    out_specs = (P(("snd", "map"), None), P("snd", "map"), P(), P())
    return jax.shard_map(shards, mesh=mesh, in_specs=in_specs, out_specs=out_specs, check_vma=False)
```

```python
import jax
import jax.numpy as jnp
from jax import lax
from jax.sharding import PartitionSpec as P
from jax.experimental import pallas as pl
from jax.experimental.pallas import tpu as pltpu

BASELINE_CELSIUS = 15.0
LOG_BASE_Q = 0.6931471805599453
PRIOR_VAR = 0.09


def ground_efflux_forward(
    ground_warmth_celsius,
    wetness_factor,
    carbon_reservoirs,
    location_category,
    category_sensitivity_effect,
    reservoir_decay_effect,
):
    nclass = category_sensitivity_effect.shape[0]
    category_onehot = (
        location_category[None, :] == jnp.arange(nclass, dtype=jnp.int32)[:, None]
    ).astype(jnp.float32)
    log_q = (
        LOG_BASE_Q
        + jnp.dot(
            category_sensitivity_effect[None, :], category_onehot, precision=lax.Precision.HIGHEST
        )[0]
    )
    base = jnp.array([0.6, 0.25, 0.1], dtype=jnp.float32)
    rates = base[:, None] * jnp.exp(
        jnp.dot(reservoir_decay_effect, category_onehot, precision=lax.Precision.HIGHEST)
    )
    decay_lifetime = (ground_warmth_celsius - BASELINE_CELSIUS) / 10.0
    modifier = jnp.exp(log_q[None, :] * decay_lifetime) * wetness_factor
    device_number = (rates * carbon_reservoirs)[:, None, :] * modifier[None]
    return (category_onehot, decay_lifetime, device_number)


def _fields_kernel(cse_ref, rde_ref, cat_ref, warm_ref, wet_ref, carbon_ref, out_ref):
    nclass = cse_ref.shape[0]
    cat = cat_ref[...]
    picked_q = jnp.zeros(cat.shape, jnp.float32)
    picked = [jnp.zeros(cat.shape, jnp.float32) for _ in range(3)]
    for c in range(nclass):
        hit = cat == c
        picked_q = jnp.where(hit, cse_ref[c], picked_q)
        for p in range(3):
            picked[p] = jnp.where(hit, rde_ref[p, c], picked[p])
    log_q = LOG_BASE_Q + picked_q
    base = (0.6, 0.25, 0.1)
    held = [base[p] * jnp.exp(picked[p]) * carbon_ref[p : p + 1, :] for p in range(3)]
    category = cat.astype(jnp.float32)
    for t in range(warm_ref.shape[0]):
        tau = (warm_ref[t : t + 1, :] - BASELINE_CELSIUS) / 10.0
        modifier = jnp.exp(log_q * tau) * wet_ref[t : t + 1, :]
        parts = [held[p] * modifier for p in range(3)]
        flux = parts[0] + parts[1] + parts[2]
        fields = (
            flux.astype(jnp.bfloat16).astype(jnp.float32),
            flux * tau,
            parts[0],
            parts[1],
            parts[2],
            category,
        )
        for q, value in enumerate(fields):
            out_ref[q, t : t + 1, :] = value


def owner_fields(
    ground_warmth_celsius,
    wetness_factor,
    carbon_reservoirs,
    location_category,
    category_sensitivity_effect,
    reservoir_decay_effect,
):
    epochs, cells = ground_warmth_celsius.shape
    smem = pl.BlockSpec(memory_space=pltpu.SMEM)
    vmem = pl.BlockSpec(memory_space=pltpu.VMEM)
    return pl.pallas_call(
        _fields_kernel,
        out_shape=jax.ShapeDtypeStruct((6, epochs, cells), jnp.float32),
        in_specs=[smem, smem, vmem, vmem, vmem, vmem],
        out_specs=vmem,
    )(
        category_sensitivity_effect,
        reservoir_decay_effect,
        location_category.reshape(1, cells),
        ground_warmth_celsius,
        wetness_factor,
        carbon_reservoirs,
    )


def shards(
    sensitivity_blocks,
    block_placement_table,
    needed_tile_lists,
    location_category,
    ground_warmth_celsius,
    wetness_factor,
    carbon_reservoirs,
    category_sensitivity_effect,
    reservoir_decay_effect,
    measured_anomaly,
    retrieval_precision,
):
    tile = sensitivity_blocks.shape[1]
    epochs_each_device, locations_each_device = ground_warmth_celsius.shape
    tiles_dev = locations_each_device // tile
    local_ids = epochs_each_device * tiles_dev
    n_snd = lax.axis_size("snd")
    n_map = lax.axis_size("map")
    cap = needed_tile_lists.shape[1]
    rows_own = measured_anomaly.shape[0]
    rows_dev = rows_own * n_map
    lanes = jnp.pad(needed_tile_lists, ((0, 0), (0, tile - cap)))[:, None, :]
    requests = lax.all_to_all(lanes, "snd", 0, 0)[:, 0, :cap]
    live = requests >= 0
    nclass = category_sensitivity_effect.shape[0]
    own_fields = owner_fields(
        ground_warmth_celsius,
        wetness_factor,
        carbon_reservoirs,
        location_category,
        category_sensitivity_effect,
        reservoir_decay_effect,
    ).reshape(6, local_ids, tile)
    asked = (
        requests.reshape(-1)[:, None] == jnp.arange(local_ids, dtype=jnp.int32)[None, :]
    ).astype(jnp.float32)
    answer = jnp.einsum("rl,qlc->rqc", asked, own_fields, precision=lax.Precision.HIGHEST)
    answer, block_placement_table, needed_tile_lists = lax.optimization_barrier(
        (answer, block_placement_table, needed_tile_lists)
    )
    received = lax.all_to_all(answer.reshape(n_snd, cap * 6, tile), "snd", 0, 0).reshape(
        n_snd * cap, 6, tile
    )

    block_row = block_placement_table[0]
    block_tile = block_placement_table[1]
    block_slot = block_placement_table[2]
    owner = block_slot // epochs_each_device
    wanted = (block_slot % epochs_each_device) * tiles_dev + block_tile
    listed = needed_tile_lists.at[owner].get(mode="promise_in_bounds")
    within = jnp.argmax(listed == wanted[:, None], axis=1).astype(jnp.int32)
    position = owner * cap + within
    vectors = received[:, 0].at[position].get(mode="promise_in_bounds")
    vectors = vectors.astype(jnp.bfloat16)
    contrib = jnp.einsum(
        "bij,bj->bi", sensitivity_blocks, vectors, preferred_element_type=jnp.float32
    )
    row_hot = (jnp.arange(rows_dev, dtype=jnp.int32)[:, None] == block_row[None, :]).astype(
        jnp.float32
    )
    partial_rows = jnp.dot(row_hot, contrib, precision=lax.Precision.HIGHEST)

    me_map = lax.axis_index("map")
    first = me_map * rows_own
    payload = jnp.concatenate([partial_rows, measured_anomaly, retrieval_precision], axis=0)
    swapped = lax.all_to_all(
        jnp.broadcast_to(payload[None], (n_map,) + payload.shape), "map", 0, 0
    )
    model_rows = jnp.sum(swapped[:, :rows_dev], axis=0)
    anomaly_rows = swapped[:, rows_dev : rows_dev + rows_own].reshape(rows_dev, tile)
    precision_rows = swapped[:, rows_dev + rows_own :].reshape(rows_dev, tile)
    diff_rows = model_rows - anomaly_rows
    weighted_rows = (diff_rows * precision_rows).astype(jnp.bfloat16)
    model_xco2 = lax.dynamic_slice(model_rows, (first, 0), (rows_own, tile))
    shard_misfit = 0.5 * jnp.sum(precision_rows * diff_rows * diff_rows)
    misfit = jnp.where(me_map == 0, shard_misfit, 0.0)

    back_rows = weighted_rows.at[block_row].get(mode="promise_in_bounds")
    block_grads = jnp.einsum(
        "bij,bi->bj", sensitivity_blocks, back_rows, preferred_element_type=jnp.float32
    )
    outgoing = jax.ops.segment_sum(
        block_grads, position, num_segments=n_snd * cap, mode="promise_in_bounds"
    )

    class_hot = (
        received[:, 5][:, :, None] == jnp.arange(nclass, dtype=jnp.float32)[None, None, :]
    ).astype(jnp.float32)
    weighted_fields = outgoing[:, None, :] * received[:, 1:5]
    class_part = jnp.einsum(
        "pqc,pck->qk", weighted_fields, class_hot, precision=lax.Precision.HIGHEST
    )
    prior = (
        jnp.concatenate([category_sensitivity_effect[None, :], reservoir_decay_effect], axis=0)
        / PRIOR_VAR
    )
    prior_cost = (
        0.5 * jnp.sum(category_sensitivity_effect * category_sensitivity_effect) / PRIOR_VAR
        + 0.5 * jnp.sum(reservoir_decay_effect * reservoir_decay_effect) / PRIOR_VAR
    )
    first_device = (me_map == 0) & (lax.axis_index("snd") == 0)
    priors = jnp.where(first_device, jnp.concatenate([prior.reshape(-1), prior_cost[None]]), 0.0)
    mine = jnp.concatenate([class_part.reshape(-1), misfit[None]]) + priors
    width = mine.shape[0]
    mine = jnp.pad(mine, (0, tile - width))
    parcel = jnp.concatenate(
        [
            outgoing.reshape(n_snd, cap, tile),
            jnp.broadcast_to(mine[None, None], (n_snd, 1, tile)),
        ],
        axis=1,
    )
    incoming = lax.all_to_all(parcel, "snd", 0, 0)
    column = jnp.sum(incoming[:, cap], axis=0)
    gathered = lax.all_to_all(jnp.broadcast_to(column[None], (n_map, tile)), "map", 0, 0)
    totals = jnp.sum(gathered, axis=0)[:width]

    target = jnp.where(live, requests, local_ids).reshape(-1)
    grad_tiles = jax.ops.segment_sum(
        incoming[:, :cap].reshape(n_snd * cap, tile),
        target,
        num_segments=local_ids + 1,
        mode="promise_in_bounds",
    )[:local_ids]
    flux_grad = grad_tiles.reshape(epochs_each_device, locations_each_device)

    class_grad = totals[:-1].reshape(4, nclass)
    cost = totals[-1]
    return (model_xco2, flux_grad, class_grad, cost)


def solution(mesh):
    in_specs = (
        P(("snd", "map"), None, None),
        P(None, ("snd", "map")),
        P(("snd", "map"), None),
        P("map"),
        P("snd", "map"),
        P("snd", "map"),
        P(None, "map"),
        P(),
        P(),
        P(("snd", "map"), None),
        P(("snd", "map"), None),
    )
    out_specs = (P(("snd", "map"), None), P("snd", "map"), P(), P())
    return jax.shard_map(shards, mesh=mesh, in_specs=in_specs, out_specs=out_specs, check_vma=False)
```

```python
import jax
import jax.numpy as jnp
from jax import lax
from jax.sharding import PartitionSpec as P
from jax.experimental import pallas as pl
from jax.experimental.pallas import tpu as pltpu

BASELINE_CELSIUS = 15.0
LOG_BASE_Q = 0.6931471805599453
PRIOR_VAR = 0.09


def ground_efflux_forward(
    ground_warmth_celsius,
    wetness_factor,
    carbon_reservoirs,
    location_category,
    category_sensitivity_effect,
    reservoir_decay_effect,
):
    nclass = category_sensitivity_effect.shape[0]
    category_onehot = (
        location_category[None, :] == jnp.arange(nclass, dtype=jnp.int32)[:, None]
    ).astype(jnp.float32)
    log_q = (
        LOG_BASE_Q
        + jnp.dot(
            category_sensitivity_effect[None, :], category_onehot, precision=lax.Precision.HIGHEST
        )[0]
    )
    base = jnp.array([0.6, 0.25, 0.1], dtype=jnp.float32)
    rates = base[:, None] * jnp.exp(
        jnp.dot(reservoir_decay_effect, category_onehot, precision=lax.Precision.HIGHEST)
    )
    decay_lifetime = (ground_warmth_celsius - BASELINE_CELSIUS) / 10.0
    modifier = jnp.exp(log_q[None, :] * decay_lifetime) * wetness_factor
    device_number = (rates * carbon_reservoirs)[:, None, :] * modifier[None]
    return (category_onehot, decay_lifetime, device_number)


def _fields_kernel(cse_ref, rde_ref, cat_ref, warm_ref, wet_ref, carbon_ref, out_ref):
    nclass = cse_ref.shape[0]
    cat = cat_ref[...]
    picked_q = jnp.zeros(cat.shape, jnp.float32)
    picked = [jnp.zeros(cat.shape, jnp.float32) for _ in range(3)]
    for c in range(nclass):
        hit = cat == c
        picked_q = jnp.where(hit, cse_ref[c], picked_q)
        for p in range(3):
            picked[p] = jnp.where(hit, rde_ref[p, c], picked[p])
    log_q = LOG_BASE_Q + picked_q
    base = (0.6, 0.25, 0.1)
    held = [base[p] * jnp.exp(picked[p]) * carbon_ref[p : p + 1, :] for p in range(3)]
    category = cat.astype(jnp.float32)
    for t in range(warm_ref.shape[0]):
        tau = (warm_ref[t : t + 1, :] - BASELINE_CELSIUS) / 10.0
        modifier = jnp.exp(log_q * tau) * wet_ref[t : t + 1, :]
        parts = [held[p] * modifier for p in range(3)]
        flux = parts[0] + parts[1] + parts[2]
        fields = (
            flux.astype(jnp.bfloat16).astype(jnp.float32),
            flux * tau,
            parts[0],
            parts[1],
            parts[2],
            category,
        )
        for q, value in enumerate(fields):
            out_ref[q, t : t + 1, :] = value


def owner_fields(
    ground_warmth_celsius,
    wetness_factor,
    carbon_reservoirs,
    location_category,
    category_sensitivity_effect,
    reservoir_decay_effect,
):
    epochs, cells = ground_warmth_celsius.shape
    smem = pl.BlockSpec(memory_space=pltpu.SMEM)
    vmem = pl.BlockSpec(memory_space=pltpu.VMEM)
    return pl.pallas_call(
        _fields_kernel,
        out_shape=jax.ShapeDtypeStruct((6, epochs, cells), jnp.float32),
        in_specs=[smem, smem, vmem, vmem, vmem, vmem],
        out_specs=vmem,
    )(
        category_sensitivity_effect,
        reservoir_decay_effect,
        location_category.reshape(1, cells),
        ground_warmth_celsius,
        wetness_factor,
        carbon_reservoirs,
    )


def shards(
    sensitivity_blocks,
    block_placement_table,
    needed_tile_lists,
    location_category,
    ground_warmth_celsius,
    wetness_factor,
    carbon_reservoirs,
    category_sensitivity_effect,
    reservoir_decay_effect,
    measured_anomaly,
    retrieval_precision,
):
    tile = sensitivity_blocks.shape[1]
    epochs_each_device, locations_each_device = ground_warmth_celsius.shape
    tiles_dev = locations_each_device // tile
    local_ids = epochs_each_device * tiles_dev
    n_snd = lax.axis_size("snd")
    n_map = lax.axis_size("map")
    cap = needed_tile_lists.shape[1]
    rows_own = measured_anomaly.shape[0]
    rows_dev = rows_own * n_map
    lanes = jnp.pad(needed_tile_lists, ((0, 0), (0, tile - cap)))[:, None, :]
    requests = lax.all_to_all(lanes, "snd", 0, 0)[:, 0, :cap]
    live = requests >= 0
    nclass = category_sensitivity_effect.shape[0]
    own_fields = owner_fields(
        ground_warmth_celsius,
        wetness_factor,
        carbon_reservoirs,
        location_category,
        category_sensitivity_effect,
        reservoir_decay_effect,
    ).reshape(6, local_ids, tile)
    asked = (
        requests.reshape(-1)[:, None] == jnp.arange(local_ids, dtype=jnp.int32)[None, :]
    ).astype(jnp.float32)
    answer = jnp.einsum("rl,qlc->rqc", asked, own_fields, precision=lax.Precision.HIGHEST)
    answer, block_placement_table, needed_tile_lists = lax.optimization_barrier(
        (answer, block_placement_table, needed_tile_lists)
    )
    received = lax.all_to_all(answer.reshape(n_snd, cap * 6, tile), "snd", 0, 0).reshape(
        n_snd * cap, 6, tile
    )

    block_row = block_placement_table[0]
    block_tile = block_placement_table[1]
    block_slot = block_placement_table[2]
    owner = block_slot // epochs_each_device
    wanted = (block_slot % epochs_each_device) * tiles_dev + block_tile
    listed = needed_tile_lists.at[owner].get(mode="promise_in_bounds")
    within = jnp.argmax(listed == wanted[:, None], axis=1).astype(jnp.int32)
    position = owner * cap + within
    vectors = received[:, 0].at[position].get(mode="promise_in_bounds")
    vectors = vectors.astype(jnp.bfloat16)
    contrib = jnp.einsum(
        "bij,bj->bi", sensitivity_blocks, vectors, preferred_element_type=jnp.float32
    )
    row_hot = (jnp.arange(rows_dev, dtype=jnp.int32)[:, None] == block_row[None, :]).astype(
        jnp.float32
    )
    partial_rows = jnp.dot(row_hot, contrib, precision=lax.Precision.HIGHEST)

    me_map = lax.axis_index("map")
    first = me_map * rows_own
    payload = jnp.concatenate([partial_rows, measured_anomaly, retrieval_precision], axis=0)
    swapped = lax.all_to_all(
        jnp.broadcast_to(payload[None], (n_map,) + payload.shape), "map", 0, 0
    )
    model_rows = jnp.sum(swapped[:, :rows_dev], axis=0)
    anomaly_rows = swapped[:, rows_dev : rows_dev + rows_own].reshape(rows_dev, tile)
    precision_rows = swapped[:, rows_dev + rows_own :].reshape(rows_dev, tile)
    diff_rows = model_rows - anomaly_rows
    weighted_rows = (diff_rows * precision_rows).astype(jnp.bfloat16)
    model_xco2 = lax.dynamic_slice(model_rows, (first, 0), (rows_own, tile))
    shard_misfit = 0.5 * jnp.sum(precision_rows * diff_rows * diff_rows)
    misfit = jnp.where(me_map == 0, shard_misfit, 0.0)

    back_rows = weighted_rows.at[block_row].get(mode="promise_in_bounds")
    block_grads = jnp.einsum(
        "bij,bi->bj", sensitivity_blocks, back_rows, preferred_element_type=jnp.float32
    )
    outgoing = jax.ops.segment_sum(
        block_grads, position, num_segments=n_snd * cap, mode="promise_in_bounds"
    )

    class_hot = (
        received[:, 5][:, :, None] == jnp.arange(nclass, dtype=jnp.float32)[None, None, :]
    ).astype(jnp.float32)
    weighted_fields = outgoing[:, None, :] * received[:, 1:5]
    class_part = jnp.einsum(
        "pqc,pck->qk", weighted_fields, class_hot, precision=lax.Precision.HIGHEST
    )
    prior = (
        jnp.concatenate([category_sensitivity_effect[None, :], reservoir_decay_effect], axis=0)
        / PRIOR_VAR
    )
    prior_cost = (
        0.5 * jnp.sum(category_sensitivity_effect * category_sensitivity_effect) / PRIOR_VAR
        + 0.5 * jnp.sum(reservoir_decay_effect * reservoir_decay_effect) / PRIOR_VAR
    )
    first_device = (me_map == 0) & (lax.axis_index("snd") == 0)
    class_rows = class_part + jnp.where(first_device, prior, 0.0)
    cost_part = misfit + jnp.where(first_device, prior_cost, 0.0)
    mine = jnp.concatenate(
        [
            jnp.pad(class_rows, ((0, 0), (0, tile - nclass))),
            jnp.pad(cost_part[None, None], ((0, 0), (0, tile - 1))),
        ],
        axis=0,
    )
    sums = mine.shape[0]
    parcel = jnp.concatenate(
        [
            outgoing.reshape(n_snd, cap, tile),
            jnp.broadcast_to(mine[None], (n_snd, sums, tile)),
        ],
        axis=1,
    )
    incoming = lax.all_to_all(parcel, "snd", 0, 0)
    column = jnp.sum(incoming[:, cap:], axis=0)
    gathered = lax.all_to_all(
        jnp.broadcast_to(column[None], (n_map, sums, tile)), "map", 0, 0
    )
    totals = jnp.sum(gathered, axis=0)
    class_grad = totals[: sums - 1, :nclass]
    cost = totals[sums - 1, 0]

    target = jnp.where(live, requests, local_ids).reshape(-1)
    grad_tiles = jax.ops.segment_sum(
        incoming[:, :cap].reshape(n_snd * cap, tile),
        target,
        num_segments=local_ids + 1,
        mode="promise_in_bounds",
    )[:local_ids]
    flux_grad = grad_tiles.reshape(epochs_each_device, locations_each_device)

    return (model_xco2, flux_grad, class_grad, cost)


def solution(mesh):
    in_specs = (
        P(("snd", "map"), None, None),
        P(None, ("snd", "map")),
        P(("snd", "map"), None),
        P("map"),
        P("snd", "map"),
        P("snd", "map"),
        P(None, "map"),
        P(),
        P(),
        P(("snd", "map"), None),
        P(("snd", "map"), None),
    )
    out_specs = (P(("snd", "map"), None), P("snd", "map"), P(), P())
    return jax.shard_map(shards, mesh=mesh, in_specs=in_specs, out_specs=out_specs, check_vma=False)
```

```python
import jax
import jax.numpy as jnp
from jax import lax
from jax.sharding import PartitionSpec as P
from jax.experimental import pallas as pl
from jax.experimental.pallas import tpu as pltpu

BASELINE_CELSIUS = 15.0
LOG_BASE_Q = 0.6931471805599453
PRIOR_VAR = 0.09


def ground_efflux_forward(
    ground_warmth_celsius,
    wetness_factor,
    carbon_reservoirs,
    location_category,
    category_sensitivity_effect,
    reservoir_decay_effect,
):
    nclass = category_sensitivity_effect.shape[0]
    category_onehot = (
        location_category[None, :] == jnp.arange(nclass, dtype=jnp.int32)[:, None]
    ).astype(jnp.float32)
    log_q = (
        LOG_BASE_Q
        + jnp.dot(
            category_sensitivity_effect[None, :], category_onehot, precision=lax.Precision.HIGHEST
        )[0]
    )
    base = jnp.array([0.6, 0.25, 0.1], dtype=jnp.float32)
    rates = base[:, None] * jnp.exp(
        jnp.dot(reservoir_decay_effect, category_onehot, precision=lax.Precision.HIGHEST)
    )
    decay_lifetime = (ground_warmth_celsius - BASELINE_CELSIUS) / 10.0
    modifier = jnp.exp(log_q[None, :] * decay_lifetime) * wetness_factor
    device_number = (rates * carbon_reservoirs)[:, None, :] * modifier[None]
    return (category_onehot, decay_lifetime, device_number)


def _fields_kernel(cse_ref, rde_ref, cat_ref, warm_ref, wet_ref, carbon_ref, out_ref):
    nclass = cse_ref.shape[0]
    cat = cat_ref[...]
    picked_q = jnp.zeros(cat.shape, jnp.float32)
    picked = [jnp.zeros(cat.shape, jnp.float32) for _ in range(3)]
    for c in range(nclass):
        hit = cat == c
        picked_q = jnp.where(hit, cse_ref[c], picked_q)
        for p in range(3):
            picked[p] = jnp.where(hit, rde_ref[p, c], picked[p])
    log_q = LOG_BASE_Q + picked_q
    base = (0.6, 0.25, 0.1)
    held = [base[p] * jnp.exp(picked[p]) * carbon_ref[p : p + 1, :] for p in range(3)]
    category = cat.astype(jnp.float32)
    for t in range(warm_ref.shape[0]):
        tau = (warm_ref[t : t + 1, :] - BASELINE_CELSIUS) / 10.0
        modifier = jnp.exp(log_q * tau) * wet_ref[t : t + 1, :]
        parts = [held[p] * modifier for p in range(3)]
        flux = parts[0] + parts[1] + parts[2]
        fields = (
            flux.astype(jnp.bfloat16).astype(jnp.float32),
            flux * tau,
            parts[0],
            parts[1],
            parts[2],
            category,
        )
        for q, value in enumerate(fields):
            out_ref[q, t : t + 1, :] = value


def owner_fields(
    ground_warmth_celsius,
    wetness_factor,
    carbon_reservoirs,
    location_category,
    category_sensitivity_effect,
    reservoir_decay_effect,
):
    epochs, cells = ground_warmth_celsius.shape
    smem = pl.BlockSpec(memory_space=pltpu.SMEM)
    vmem = pl.BlockSpec(memory_space=pltpu.VMEM)
    return pl.pallas_call(
        _fields_kernel,
        out_shape=jax.ShapeDtypeStruct((6, epochs, cells), jnp.float32),
        in_specs=[smem, smem, vmem, vmem, vmem, vmem],
        out_specs=vmem,
    )(
        category_sensitivity_effect,
        reservoir_decay_effect,
        location_category.reshape(1, cells),
        ground_warmth_celsius,
        wetness_factor,
        carbon_reservoirs,
    )


def shards(
    sensitivity_blocks,
    block_placement_table,
    needed_tile_lists,
    location_category,
    ground_warmth_celsius,
    wetness_factor,
    carbon_reservoirs,
    category_sensitivity_effect,
    reservoir_decay_effect,
    measured_anomaly,
    retrieval_precision,
):
    tile = sensitivity_blocks.shape[1]
    epochs_each_device, locations_each_device = ground_warmth_celsius.shape
    tiles_dev = locations_each_device // tile
    local_ids = epochs_each_device * tiles_dev
    n_snd = lax.axis_size("snd")
    n_map = lax.axis_size("map")
    cap = needed_tile_lists.shape[1]
    rows_own = measured_anomaly.shape[0]
    rows_dev = rows_own * n_map
    spread = jnp.eye(cap, tile, dtype=jnp.float32)
    lanes = jnp.dot(
        needed_tile_lists.astype(jnp.float32), spread, precision=lax.Precision.HIGHEST
    )
    requests = lax.all_to_all(lanes[:, None, :], "snd", 0, 0)[:, 0, :cap].astype(jnp.int32)
    live = requests >= 0
    nclass = category_sensitivity_effect.shape[0]
    own_fields = owner_fields(
        ground_warmth_celsius,
        wetness_factor,
        carbon_reservoirs,
        location_category,
        category_sensitivity_effect,
        reservoir_decay_effect,
    ).reshape(6, local_ids, tile)
    asked = (
        requests.reshape(-1)[:, None] == jnp.arange(local_ids, dtype=jnp.int32)[None, :]
    ).astype(jnp.float32)
    answer = jnp.einsum("rl,qlc->rqc", asked, own_fields, precision=lax.Precision.HIGHEST)
    answer, block_placement_table, needed_tile_lists = lax.optimization_barrier(
        (answer, block_placement_table, needed_tile_lists)
    )
    received = lax.all_to_all(answer.reshape(n_snd, cap * 6, tile), "snd", 0, 0).reshape(
        n_snd * cap, 6, tile
    )

    block_row = block_placement_table[0]
    block_tile = block_placement_table[1]
    block_slot = block_placement_table[2]
    owner = block_slot // epochs_each_device
    wanted = (block_slot % epochs_each_device) * tiles_dev + block_tile
    listed = needed_tile_lists.at[owner].get(mode="promise_in_bounds")
    within = jnp.argmax(listed == wanted[:, None], axis=1).astype(jnp.int32)
    position = owner * cap + within
    vectors = received[:, 0].at[position].get(mode="promise_in_bounds")
    vectors = vectors.astype(jnp.bfloat16)
    contrib = jnp.einsum(
        "bij,bj->bi", sensitivity_blocks, vectors, preferred_element_type=jnp.float32
    )
    row_hot = (jnp.arange(rows_dev, dtype=jnp.int32)[:, None] == block_row[None, :]).astype(
        jnp.float32
    )
    partial_rows = jnp.dot(row_hot, contrib, precision=lax.Precision.HIGHEST)

    me_map = lax.axis_index("map")
    first = me_map * rows_own
    payload = jnp.concatenate([partial_rows, measured_anomaly, retrieval_precision], axis=0)
    swapped = lax.all_to_all(
        jnp.broadcast_to(payload[None], (n_map,) + payload.shape), "map", 0, 0
    )
    model_rows = jnp.sum(swapped[:, :rows_dev], axis=0)
    anomaly_rows = swapped[:, rows_dev : rows_dev + rows_own].reshape(rows_dev, tile)
    precision_rows = swapped[:, rows_dev + rows_own :].reshape(rows_dev, tile)
    diff_rows = model_rows - anomaly_rows
    weighted_rows = (diff_rows * precision_rows).astype(jnp.bfloat16)
    model_xco2 = lax.dynamic_slice(model_rows, (first, 0), (rows_own, tile))
    shard_misfit = 0.5 * jnp.sum(precision_rows * diff_rows * diff_rows)
    misfit = jnp.where(me_map == 0, shard_misfit, 0.0)

    back_rows = weighted_rows.at[block_row].get(mode="promise_in_bounds")
    block_grads = jnp.einsum(
        "bij,bi->bj", sensitivity_blocks, back_rows, preferred_element_type=jnp.float32
    )
    outgoing = jax.ops.segment_sum(
        block_grads, position, num_segments=n_snd * cap, mode="promise_in_bounds"
    )

    class_hot = (
        received[:, 5][:, :, None] == jnp.arange(nclass, dtype=jnp.float32)[None, None, :]
    ).astype(jnp.float32)
    weighted_fields = outgoing[:, None, :] * received[:, 1:5]
    class_part = jnp.einsum(
        "pqc,pck->qk", weighted_fields, class_hot, precision=lax.Precision.HIGHEST
    )
    prior = (
        jnp.concatenate([category_sensitivity_effect[None, :], reservoir_decay_effect], axis=0)
        / PRIOR_VAR
    )
    prior_cost = (
        0.5 * jnp.sum(category_sensitivity_effect * category_sensitivity_effect) / PRIOR_VAR
        + 0.5 * jnp.sum(reservoir_decay_effect * reservoir_decay_effect) / PRIOR_VAR
    )
    first_device = (me_map == 0) & (lax.axis_index("snd") == 0)
    priors = jnp.where(first_device, jnp.concatenate([prior.reshape(-1), prior_cost[None]]), 0.0)
    mine = jnp.concatenate([class_part.reshape(-1), misfit[None]]) + priors
    width = mine.shape[0]
    mine = jnp.pad(mine, (0, tile - width))
    parcel = jnp.concatenate(
        [
            outgoing.reshape(n_snd, cap, tile),
            jnp.broadcast_to(mine[None, None], (n_snd, 1, tile)),
        ],
        axis=1,
    )
    incoming = lax.all_to_all(parcel, "snd", 0, 0)
    column = jnp.sum(incoming[:, cap], axis=0)
    gathered = lax.all_to_all(jnp.broadcast_to(column[None], (n_map, tile)), "map", 0, 0)
    totals = jnp.sum(gathered, axis=0)[:width]

    target = jnp.where(live, requests, local_ids).reshape(-1)
    grad_tiles = jax.ops.segment_sum(
        incoming[:, :cap].reshape(n_snd * cap, tile),
        target,
        num_segments=local_ids + 1,
        mode="promise_in_bounds",
    )[:local_ids]
    flux_grad = grad_tiles.reshape(epochs_each_device, locations_each_device)

    class_grad = totals[:-1].reshape(4, nclass)
    cost = totals[-1]
    return (model_xco2, flux_grad, class_grad, cost)


def solution(mesh):
    in_specs = (
        P(("snd", "map"), None, None),
        P(None, ("snd", "map")),
        P(("snd", "map"), None),
        P("map"),
        P("snd", "map"),
        P("snd", "map"),
        P(None, "map"),
        P(),
        P(),
        P(("snd", "map"), None),
        P(("snd", "map"), None),
    )
    out_specs = (P(("snd", "map"), None), P("snd", "map"), P(), P())
    return jax.shard_map(shards, mesh=mesh, in_specs=in_specs, out_specs=out_specs, check_vma=False)
```

```python
import jax
import jax.numpy as jnp
from jax import lax
from jax.sharding import PartitionSpec as P
from jax.experimental import pallas as pl
from jax.experimental.pallas import tpu as pltpu

BASELINE_CELSIUS = 15.0
LOG_BASE_Q = 0.6931471805599453
PRIOR_VAR = 0.09


def ground_efflux_forward(
    ground_warmth_celsius,
    wetness_factor,
    carbon_reservoirs,
    location_category,
    category_sensitivity_effect,
    reservoir_decay_effect,
):
    nclass = category_sensitivity_effect.shape[0]
    category_onehot = (
        location_category[None, :] == jnp.arange(nclass, dtype=jnp.int32)[:, None]
    ).astype(jnp.float32)
    log_q = (
        LOG_BASE_Q
        + jnp.dot(
            category_sensitivity_effect[None, :], category_onehot, precision=lax.Precision.HIGHEST
        )[0]
    )
    base = jnp.array([0.6, 0.25, 0.1], dtype=jnp.float32)
    rates = base[:, None] * jnp.exp(
        jnp.dot(reservoir_decay_effect, category_onehot, precision=lax.Precision.HIGHEST)
    )
    decay_lifetime = (ground_warmth_celsius - BASELINE_CELSIUS) / 10.0
    modifier = jnp.exp(log_q[None, :] * decay_lifetime) * wetness_factor
    device_number = (rates * carbon_reservoirs)[:, None, :] * modifier[None]
    return (category_onehot, decay_lifetime, device_number)


def _fields_kernel(cse_ref, rde_ref, cat_ref, warm_ref, wet_ref, carbon_ref, out_ref):
    nclass = cse_ref.shape[0]
    cat = cat_ref[...]
    picked_q = jnp.zeros(cat.shape, jnp.float32)
    picked = [jnp.zeros(cat.shape, jnp.float32) for _ in range(3)]
    for c in range(nclass):
        hit = cat == c
        picked_q = jnp.where(hit, cse_ref[c], picked_q)
        for p in range(3):
            picked[p] = jnp.where(hit, rde_ref[p, c], picked[p])
    log_q = LOG_BASE_Q + picked_q
    base = (0.6, 0.25, 0.1)
    held = [base[p] * jnp.exp(picked[p]) * carbon_ref[p : p + 1, :] for p in range(3)]
    category = cat.astype(jnp.float32)
    for t in range(warm_ref.shape[0]):
        tau = (warm_ref[t : t + 1, :] - BASELINE_CELSIUS) / 10.0
        modifier = jnp.exp(log_q * tau) * wet_ref[t : t + 1, :]
        parts = [held[p] * modifier for p in range(3)]
        flux = parts[0] + parts[1] + parts[2]
        fields = (
            flux.astype(jnp.bfloat16).astype(jnp.float32),
            flux * tau,
            parts[0],
            parts[1],
            parts[2],
            category,
        )
        for q, value in enumerate(fields):
            out_ref[q, t : t + 1, :] = value


def owner_fields(
    ground_warmth_celsius,
    wetness_factor,
    carbon_reservoirs,
    location_category,
    category_sensitivity_effect,
    reservoir_decay_effect,
):
    epochs, cells = ground_warmth_celsius.shape
    smem = pl.BlockSpec(memory_space=pltpu.SMEM)
    vmem = pl.BlockSpec(memory_space=pltpu.VMEM)
    return pl.pallas_call(
        _fields_kernel,
        out_shape=jax.ShapeDtypeStruct((6, epochs, cells), jnp.float32),
        in_specs=[smem, smem, vmem, vmem, vmem, vmem],
        out_specs=vmem,
    )(
        category_sensitivity_effect,
        reservoir_decay_effect,
        location_category.reshape(1, cells),
        ground_warmth_celsius,
        wetness_factor,
        carbon_reservoirs,
    )


def shards(
    sensitivity_blocks,
    block_placement_table,
    needed_tile_lists,
    location_category,
    ground_warmth_celsius,
    wetness_factor,
    carbon_reservoirs,
    category_sensitivity_effect,
    reservoir_decay_effect,
    measured_anomaly,
    retrieval_precision,
):
    tile = sensitivity_blocks.shape[1]
    epochs_each_device, locations_each_device = ground_warmth_celsius.shape
    tiles_dev = locations_each_device // tile
    local_ids = epochs_each_device * tiles_dev
    n_snd = lax.axis_size("snd")
    n_map = lax.axis_size("map")
    cap = needed_tile_lists.shape[1]
    rows_own = measured_anomaly.shape[0]
    rows_dev = rows_own * n_map
    lanes = jnp.pad(needed_tile_lists, ((0, 0), (0, tile - cap)))[:, None, :]
    requests = lax.all_to_all(lanes, "snd", 0, 0)[:, 0, :cap]
    live = requests >= 0
    nclass = category_sensitivity_effect.shape[0]
    own_fields = owner_fields(
        ground_warmth_celsius,
        wetness_factor,
        carbon_reservoirs,
        location_category,
        category_sensitivity_effect,
        reservoir_decay_effect,
    ).reshape(6, local_ids, tile)
    asked = (
        requests.reshape(-1)[:, None] == jnp.arange(local_ids, dtype=jnp.int32)[None, :]
    ).astype(jnp.float32)
    answer = jnp.einsum("rl,qlc->rqc", asked, own_fields, precision=lax.Precision.HIGHEST)
    answer, block_placement_table, needed_tile_lists = lax.optimization_barrier(
        (answer, block_placement_table, needed_tile_lists)
    )
    received = lax.all_to_all(answer.reshape(n_snd, cap * 6, tile), "snd", 0, 0).reshape(
        n_snd * cap, 6, tile
    )

    block_row = block_placement_table[0]
    block_tile = block_placement_table[1]
    block_slot = block_placement_table[2]
    owner = block_slot // epochs_each_device
    wanted = (block_slot % epochs_each_device) * tiles_dev + block_tile
    listed = needed_tile_lists.at[owner].get(mode="promise_in_bounds")
    within = jnp.argmax(listed == wanted[:, None], axis=1).astype(jnp.int32)
    position = owner * cap + within
    vectors = received[:, 0].at[position].get(mode="promise_in_bounds")
    vectors = vectors.astype(jnp.bfloat16)
    contrib = jnp.einsum(
        "bij,bj->bi", sensitivity_blocks, vectors, preferred_element_type=jnp.float32
    )
    row_hot = (jnp.arange(rows_dev, dtype=jnp.int32)[:, None] == block_row[None, :]).astype(
        jnp.float32
    )

    me_map = lax.axis_index("map")
    first = me_map * rows_own
    extra = 2 * rows_own
    picks = jnp.concatenate(
        [
            jnp.concatenate([row_hot, jnp.zeros((rows_dev, extra), jnp.float32)], axis=1),
            jnp.concatenate(
                [jnp.zeros((extra, row_hot.shape[1]), jnp.float32), jnp.eye(extra, dtype=jnp.float32)],
                axis=1,
            ),
        ],
        axis=0,
    )
    picks = jnp.broadcast_to(picks[None], (n_map,) + picks.shape).reshape(-1, picks.shape[1])
    sources = jnp.concatenate([contrib, measured_anomaly, retrieval_precision], axis=0)
    swapped = lax.all_to_all(
        jnp.dot(picks, sources, precision=lax.Precision.HIGHEST).reshape(n_map, -1, tile),
        "map",
        0,
        0,
    )
    model_rows = jnp.sum(swapped[:, :rows_dev], axis=0)
    anomaly_rows = swapped[:, rows_dev : rows_dev + rows_own].reshape(rows_dev, tile)
    precision_rows = swapped[:, rows_dev + rows_own :].reshape(rows_dev, tile)
    diff_rows = model_rows - anomaly_rows
    weighted_rows = (diff_rows * precision_rows).astype(jnp.bfloat16)
    model_xco2 = lax.dynamic_slice(model_rows, (first, 0), (rows_own, tile))
    shard_misfit = 0.5 * jnp.sum(precision_rows * diff_rows * diff_rows)
    misfit = jnp.where(me_map == 0, shard_misfit, 0.0)

    back_rows = weighted_rows.at[block_row].get(mode="promise_in_bounds")
    block_grads = jnp.einsum(
        "bij,bi->bj", sensitivity_blocks, back_rows, preferred_element_type=jnp.float32
    )
    outgoing = jax.ops.segment_sum(
        block_grads, position, num_segments=n_snd * cap, mode="promise_in_bounds"
    )

    class_hot = (
        received[:, 5][:, :, None] == jnp.arange(nclass, dtype=jnp.float32)[None, None, :]
    ).astype(jnp.float32)
    weighted_fields = outgoing[:, None, :] * received[:, 1:5]
    class_part = jnp.einsum(
        "pqc,pck->qk", weighted_fields, class_hot, precision=lax.Precision.HIGHEST
    )
    prior = (
        jnp.concatenate([category_sensitivity_effect[None, :], reservoir_decay_effect], axis=0)
        / PRIOR_VAR
    )
    prior_cost = (
        0.5 * jnp.sum(category_sensitivity_effect * category_sensitivity_effect) / PRIOR_VAR
        + 0.5 * jnp.sum(reservoir_decay_effect * reservoir_decay_effect) / PRIOR_VAR
    )
    first_device = (me_map == 0) & (lax.axis_index("snd") == 0)
    priors = jnp.where(first_device, jnp.concatenate([prior.reshape(-1), prior_cost[None]]), 0.0)
    mine = jnp.concatenate([class_part.reshape(-1), misfit[None]]) + priors
    width = mine.shape[0]
    mine = jnp.pad(mine, (0, tile - width))
    parcel = jnp.concatenate(
        [
            outgoing.reshape(n_snd, cap, tile),
            jnp.broadcast_to(mine[None, None], (n_snd, 1, tile)),
        ],
        axis=1,
    )
    incoming = lax.all_to_all(parcel, "snd", 0, 0)
    column = jnp.sum(incoming[:, cap], axis=0)
    gathered = lax.all_to_all(jnp.broadcast_to(column[None], (n_map, tile)), "map", 0, 0)
    totals = jnp.sum(gathered, axis=0)[:width]

    target = jnp.where(live, requests, local_ids).reshape(-1)
    grad_tiles = jax.ops.segment_sum(
        incoming[:, :cap].reshape(n_snd * cap, tile),
        target,
        num_segments=local_ids + 1,
        mode="promise_in_bounds",
    )[:local_ids]
    flux_grad = grad_tiles.reshape(epochs_each_device, locations_each_device)

    class_grad = totals[:-1].reshape(4, nclass)
    cost = totals[-1]
    return (model_xco2, flux_grad, class_grad, cost)


def solution(mesh):
    in_specs = (
        P(("snd", "map"), None, None),
        P(None, ("snd", "map")),
        P(("snd", "map"), None),
        P("map"),
        P("snd", "map"),
        P("snd", "map"),
        P(None, "map"),
        P(),
        P(),
        P(("snd", "map"), None),
        P(("snd", "map"), None),
    )
    out_specs = (P(("snd", "map"), None), P("snd", "map"), P(), P())
    return jax.shard_map(shards, mesh=mesh, in_specs=in_specs, out_specs=out_specs, check_vma=False)
```
